32 devices in a mesh: vol: 2 (over y), wide: 4 (over z), narrow: 4 (over x, core).
Axes of the slice: x: 2, y: 2, z: 4, core: 2. Of those that a mesh axis runs over, the one named last changes fastest.
Arguments:
- tiles: float32 [32, 32, 128, 128], P(('vol', 'narrow'), 'wide'), parts along dimension 0, as said below
- pattern: int32 [32, 32], P(('vol', 'narrow'), 'wide'), parts along dimension 0, may hold values from 0 to 15, as said below
- seed_label: int32 [4096, 1], P(('vol', 'narrow', 'wide')), parts along dimension 0, may hold values from 0 to 255, as said below
Outputs:
- solution: float32 [4096, 128], P(('vol', 'narrow', 'wide')), parts along dimension 0
- residual: float32 [4096, 128], P(('vol', 'narrow', 'wide')), parts along dimension 0
The draws below stay inside these ranges and needn't reach their ends.
There are 2 independent parts, one for each index of `vol`. The reference program is written for one: setup_inputs(seed, part) draws one part's arguments, and reference() takes and returns one part's arrays. A program takes and returns all parts, laid end to end along the dimension named above; each array names one. Nothing has to cross between parts.
Inputs may be any that keep to these rules, and one draw needn't show every extreme that they name: `pattern`: stored tile k of block row r lies in block column c with (c % (16 // 4)) == k // (32 // 4); every block column is named 32 times in all; W is symmetric: the tile at (r, c) is the transpose of the tile at (c, r), and a tile at (r, r) is symmetric. `tiles`: entries lie between 0 and 8, and W built from them is symmetric. `seed_label`: values under 128 are the seed label of a seeded supervoxel, values of 128 or more mark an unseeded one; exactly 128 supervoxels are seeded, and every value occurs.
All inputs are finite; a program needn't handle non-finite values.
Results may differ from the reference program's by a relative error of at most 0.0003.
Values sent between devices are 32-bit elements; how exact they have to be, the bound alone decides.
No kernel may reach another device: no remote copies, remote signals or barrier semaphores. Data moves between devices by JAX's collectives and lax.ppermute only.
A program may use at most 64 MiB of HBM per device.

```python
import jax
import jax.numpy as jnp
from jax import lax

TILE = 128
SLOTS = 32
SEED_CLASSES = 128
ITERS = 3
BR_DEV = 1
NBR = 16
NODES = 2048
N_WIDE = 4
N_NARROW = 4


def pair_table(key):
    base = jax.random.fold_in(key, 11)
    per_group = SLOTS // N_WIDE
    members = N_NARROW * BR_DEV
    row_group = BR_DEV * N_WIDE
    keys = jax.random.split(base, per_group * N_WIDE * N_WIDE)
    perms = jax.vmap(lambda one_key: jax.random.permutation(one_key, members))(keys)
    perms = perms.reshape(per_group, N_WIDE, N_WIDE, members).astype(jnp.int32)
    inverse = jnp.argsort(perms, axis=-1, stable=True).astype(jnp.int32)
    partner = jnp.take_along_axis(perms, jnp.bitwise_xor(inverse, 1), axis=-1)
    first = jnp.arange(N_WIDE, dtype=jnp.int32)[None, :, None, None]
    second = jnp.arange(N_WIDE, dtype=jnp.int32)[None, None, :, None]
    match = jnp.where(first < second, perms, jnp.where(first > second, jnp.swapaxes(inverse, 1, 2), partner))
    rows = jnp.arange(NBR, dtype=jnp.int32)
    narrow_of = rows // row_group
    wide_of = rows % row_group // BR_DEV
    member = narrow_of * BR_DEV + rows % BR_DEV
    slots = jnp.arange(SLOTS, dtype=jnp.int32)
    target = slots // per_group
    layer = slots % per_group
    chosen = match[layer[None, :], wide_of[:, None], target[None, :], member[:, None]]
    columns = chosen // BR_DEV * row_group + target[None, :] * BR_DEV + chosen % BR_DEV
    partner_slot = wide_of[:, None] * per_group + layer[None, :]
    return (columns.astype(jnp.int32), partner_slot.astype(jnp.int32))


def draw_pattern(key, part):
    columns, partner_slot = pair_table(key)
    return columns


def draw_tiles(key, part):
    columns, partner_slot = pair_table(key)
    shape_full = (NBR, SLOTS, TILE, TILE)
    density = 4.0 / (SLOTS * TILE)
    strong_part = jnp.maximum(jax.random.uniform(jax.random.fold_in(key, 23), shape_full, jnp.float32) - (1.0 - density), 0.0) / density
    weak_part = jax.random.uniform(jax.random.fold_in(key, 31), shape_full, jnp.float32) / (SLOTS * TILE)
    raw_entries = strong_part + weak_part
    mirrored = raw_entries[columns, partner_slot]
    result = (raw_entries + jnp.swapaxes(mirrored, -1, -2)) * 0.4
    return result


def draw_seed_label(key, part):
    base_key = jax.random.fold_in(key, 37)
    marked_node_count = max(SEED_CLASSES, NODES // 32)
    vertex_position = jax.random.permutation(jax.random.fold_in(base_key, 1), NODES).astype(jnp.int32)
    extra_seed = jax.random.randint(jax.random.fold_in(base_key, 2), (NODES,), 0, SEED_CLASSES, dtype=jnp.int32)
    additional_marker = jax.random.randint(jax.random.fold_in(base_key, 3), (NODES,), 0, SEED_CLASSES, dtype=jnp.int32)
    marked_node_value = jnp.where(vertex_position < SEED_CLASSES, vertex_position, extra_seed)
    unknown_node_position = vertex_position - marked_node_count
    unmarked_flag = SEED_CLASSES + jnp.where(unknown_node_position < SEED_CLASSES, unknown_node_position, additional_marker)
    entry_value = jnp.where(vertex_position < marked_node_count, marked_node_value, unmarked_flag)
    return entry_value.reshape(NODES, 1).astype(jnp.int32)


def setup_inputs(seed: int = 0, part: int = 0) -> dict:
    arg_keys = jax.random.split(jax.random.key(seed), 4)
    part_splits = jax.random.split(jax.random.fold_in(arg_keys[3], part), 4)
    return {
        "tiles": draw_tiles(jax.random.fold_in(jax.random.fold_in(arg_keys[3], part), 71), part),
        "pattern": draw_pattern(jax.random.fold_in(jax.random.fold_in(arg_keys[3], part), 71), part),
        "seed_label": draw_seed_label(jax.random.fold_in(jax.random.fold_in(arg_keys[3], part), 71), part),
    }


SEED_WEIGHT = 2.0
PRIOR = 0.5


def apply_operator(field, tiles, pattern, diag):
    blocks = field.reshape(NBR, TILE, SEED_CLASSES)

    def one_row(args):
        tile_row, column_row = args
        picked = blocks[column_row]
        return jnp.einsum("kab,kbl->al", tile_row, picked, precision=lax.Precision.HIGHEST)

    weighted = lax.map(one_row, (tiles, pattern)).reshape(NODES, SEED_CLASSES)
    return diag[:, None] * field - weighted


def reference(tiles, pattern, seed_label):
    degree = jnp.sum(tiles, axis=(1, 3)).reshape(NODES)
    labels = seed_label[:, 0]
    seeded = (labels < SEED_CLASSES).astype(jnp.float32)
    diag = degree + SEED_WEIGHT * seeded + PRIOR
    rhs = SEED_WEIGHT * (labels[:, None] == jnp.arange(SEED_CLASSES, dtype=jnp.int32)[None, :]).astype(jnp.float32)
    solution = jnp.zeros_like(rhs)
    residual = rhs
    direction = rhs
    norm_now = jnp.sum(residual * residual, axis=0)
    for step in range(ITERS):
        image = apply_operator(direction, tiles, pattern, diag)
        alpha = norm_now / jnp.sum(direction * image, axis=0)
        solution = solution + alpha * direction
        residual = residual - alpha * image
        norm_next = jnp.sum(residual * residual, axis=0)
        direction = residual + (norm_next / norm_now) * direction
        norm_now = norm_next
    return solution, residual
```

```python
import jax
import jax.numpy as jnp
from jax import lax
from jax.sharding import PartitionSpec as P

SEED_CLASSES = 128
ITERS = 3


SEED_WEIGHT = 2.0
PRIOR = 0.5


def sum_over(values, axes, count):
    spread = jnp.broadcast_to(values[None], (count,) + values.shape)
    return jnp.sum(lax.all_to_all(spread, axes, 0, 0, tiled=True), axis=0)


def scatter_sum(blocks, axis, count):
    if count > 4:
        return jnp.sum(lax.all_to_all(blocks, axis, 0, 0, tiled=True), axis=0)
    me = lax.axis_index(axis)
    total = lax.dynamic_index_in_dim(blocks, me, 0, keepdims=False)
    for shift in range(1, count):
        sent = lax.dynamic_index_in_dim(blocks, (me + shift) % count, 0, keepdims=False)
        pairs = [(i, (i + shift) % count) for i in range(count)]
        total = total + lax.ppermute(sent, axis, pairs)
    return total


def local(tiles, pattern, seed_label):
    groups = tiles.shape[0]
    tile = tiles.shape[2]
    own_rows = seed_label.shape[0]
    br_local = own_rows // tile
    n_wide = lax.axis_size("wide")
    n_all = n_wide * lax.axis_size("narrow")
    local_column = pattern // groups * br_local + pattern % br_local
    row_sums = jnp.sum(tiles, axis=(1, 3))
    degree = scatter_sum(row_sums.reshape(n_wide, own_rows), "wide", n_wide).reshape(own_rows)
    seeded = (seed_label[:, 0] < SEED_CLASSES).astype(jnp.float32)
    diag_column = (degree + SEED_WEIGHT * seeded + PRIOR)[:, None]

    def reduce_dots(values):
        return sum_over(values, ("wide", "narrow"), n_all)

    labels = seed_label[:, 0]
    rhs = SEED_WEIGHT * (
        labels[:, None] == jnp.arange(SEED_CLASSES, dtype=jnp.int32)[None, :]
    ).astype(jnp.float32)
    solution = jnp.zeros_like(rhs)
    residual = rhs
    direction = rhs
    norm_now = reduce_dots(jnp.sum(residual * residual, axis=0))
    for step in range(ITERS):
        gathered = lax.all_gather(direction, "narrow", axis=0, tiled=True)
        width = gathered.shape[1]
        blocks = gathered.reshape(-1, tile, width)
        picked = blocks[local_column]
        result = jnp.einsum("mkab,mkbl->mal", tiles, picked, precision=lax.Precision.HIGHEST)
        image = diag_column * direction - scatter_sum(
            result.reshape(n_wide, own_rows, width), "wide", n_wide
        )
        curvature = reduce_dots(jnp.sum(direction * image, axis=0))
        alpha = norm_now / curvature
        solution = solution + alpha * direction
        residual = residual - alpha * image
        norm_next = reduce_dots(jnp.sum(residual * residual, axis=0))
        direction = residual + norm_next / norm_now * direction
        norm_now = norm_next
    return (solution, residual)


def solution(mesh):
    placed = (
        P(("vol", "narrow"), "wide", None, None),
        P(("vol", "narrow"), "wide"),
        P(("vol", "narrow", "wide"), None),
    )
    return jax.shard_map(
        local,
        mesh=mesh,
        in_specs=placed,
        out_specs=(P(("vol", "narrow", "wide"), None), P(("vol", "narrow", "wide"), None)),
        check_vma=False,
    )
```

```python
import jax
import jax.numpy as jnp
from jax import lax
from jax.sharding import PartitionSpec as P

SEED_CLASSES = 128
ITERS = 3


SEED_WEIGHT = 2.0
PRIOR = 0.5


def sum_over(values, axes, count):
    spread = jnp.broadcast_to(values[None], (count,) + values.shape)
    return jnp.sum(lax.all_to_all(spread, axes, 0, 0, tiled=True), axis=0)


def scatter_sum(blocks, axis, count):
    if count > 4:
        return jnp.sum(lax.all_to_all(blocks, axis, 0, 0, tiled=True), axis=0)
    me = lax.axis_index(axis)
    total = lax.dynamic_index_in_dim(blocks, me, 0, keepdims=False)
    for shift in range(1, count):
        sent = lax.dynamic_index_in_dim(blocks, (me + shift) % count, 0, keepdims=False)
        pairs = [(i, (i + shift) % count) for i in range(count)]
        total = total + lax.ppermute(sent, axis, pairs)
    return total


def gather_blocks(values, axis, count):
    if count > 4:
        return lax.all_gather(values, axis, axis=0, tiled=False)
    parts = [values]
    for shift in range(1, count):
        pairs = [(i, (i + shift) % count) for i in range(count)]
        parts.append(lax.ppermute(values, axis, pairs))
    return jnp.stack(parts)


def local(tiles, pattern, seed_label):
    groups = tiles.shape[0]
    tile = tiles.shape[2]
    own_rows = seed_label.shape[0]
    br_local = own_rows // tile
    n_wide = lax.axis_size("wide")
    n_narrow = lax.axis_size("narrow")
    n_all = n_wide * n_narrow
    width = SEED_CLASSES
    local_column = pattern // groups * br_local + pattern % br_local
    if n_narrow > 4:
        source = local_column
    else:
        source = (lax.axis_index("narrow") - local_column) % n_narrow
    pick = source[:, :, None] == jnp.arange(n_narrow, dtype=source.dtype)[None, None, :]
    dense = jnp.sum(
        jnp.where(pick[:, :, None, :, None], tiles[:, :, :, None, :], 0.0), axis=1
    ).reshape(groups * tile, n_narrow * own_rows)

    row_sums = jnp.sum(tiles, axis=(1, 3))
    degree = scatter_sum(row_sums.reshape(n_wide, own_rows), "wide", n_wide).reshape(own_rows)
    seeded = (seed_label[:, 0] < SEED_CLASSES).astype(jnp.float32)
    diag_column = (degree + SEED_WEIGHT * seeded + PRIOR)[:, None]

    def product(values):
        gathered = gather_blocks(values, "narrow", n_narrow).reshape(n_narrow * own_rows, width)
        partial = jnp.dot(dense, gathered, precision=lax.Precision.HIGHEST)
        return scatter_sum(partial.reshape(n_wide, own_rows, width), "wide", n_wide)

    def reduce_dots(values):
        return sum_over(values, ("wide", "narrow"), n_all)

    labels = seed_label[:, 0]
    rhs = SEED_WEIGHT * (
        labels[:, None] == jnp.arange(SEED_CLASSES, dtype=jnp.int32)[None, :]
    ).astype(jnp.float32)
    solution = jnp.zeros_like(rhs)
    residual = rhs
    direction = rhs
    weighted = product(direction)
    image = diag_column * direction - weighted
    first = reduce_dots(
        jnp.stack([jnp.sum(residual * residual, axis=0), jnp.sum(direction * image, axis=0)])
    )
    norm_now = first[0]
    curvature = first[1]
    for step in range(ITERS):
        alpha = norm_now / curvature
        solution = solution + alpha * direction
        residual = residual - alpha * image
        if step == ITERS - 1:
            break
        weighted_residual = product(residual)
        norm_next = reduce_dots(jnp.sum(residual * residual, axis=0))
        ratio = norm_next / norm_now
        direction = residual + ratio * direction
        weighted = weighted_residual + ratio * weighted
        image = diag_column * direction - weighted
        curvature = reduce_dots(jnp.sum(direction * image, axis=0))
        norm_now = norm_next
    return (solution, residual)


def solution(mesh):
    placed = (
        P(("vol", "narrow"), "wide", None, None),
        P(("vol", "narrow"), "wide"),
        P(("vol", "narrow", "wide"), None),
    )
    return jax.shard_map(
        local,
        mesh=mesh,
        in_specs=placed,
        out_specs=(P(("vol", "narrow", "wide"), None), P(("vol", "narrow", "wide"), None)),
        check_vma=False,
    )
```

```python
import jax
import jax.numpy as jnp
from jax import lax
from jax.sharding import PartitionSpec as P

SEED_CLASSES = 128
ITERS = 3


SEED_WEIGHT = 2.0
PRIOR = 0.5


def sum_over(values, axes, count):
    spread = jnp.broadcast_to(values[None], (count,) + values.shape)
    return jnp.sum(lax.all_to_all(spread, axes, 0, 0, tiled=True), axis=0)


def scatter_sum(blocks, axis, count):
    if count > 4:
        return jnp.sum(lax.all_to_all(blocks, axis, 0, 0, tiled=True), axis=0)
    me = lax.axis_index(axis)
    total = lax.dynamic_index_in_dim(blocks, me, 0, keepdims=False)
    for shift in range(1, count):
        sent = lax.dynamic_index_in_dim(blocks, (me + shift) % count, 0, keepdims=False)
        pairs = [(i, (i + shift) % count) for i in range(count)]
        total = total + lax.ppermute(sent, axis, pairs)
    return total


def gather_blocks(values, axis, count):
    if count > 4:
        return lax.all_gather(values, axis, axis=0, tiled=False)
    parts = [values]
    for shift in range(1, count):
        pairs = [(i, (i + shift) % count) for i in range(count)]
        parts.append(lax.ppermute(values, axis, pairs))
    return jnp.stack(parts)


def source(axis, count, entry):
    if count > 4:
        return entry
    return (lax.axis_index(axis) - entry) % count


def local(tiles, pattern, seed_label):
    groups = tiles.shape[0]
    tile = tiles.shape[2]
    own_rows = seed_label.shape[0]
    br_local = own_rows // tile
    n_wide = lax.axis_size("wide")
    n_narrow = lax.axis_size("narrow")
    n_all = n_wide * n_narrow
    width = SEED_CLASSES
    local_column = pattern // groups * br_local + pattern % br_local
    entries = jnp.arange(n_narrow, dtype=local_column.dtype)
    pick = local_column[:, :, None] == source("narrow", n_narrow, entries)[None, None, :]
    dense = jnp.sum(
        jnp.where(pick[:, :, None, :, None], tiles[:, :, :, None, :], 0.0), axis=1
    ).reshape(groups * tile, n_narrow * own_rows)

    row_sums = jnp.sum(tiles, axis=(1, 3))
    degree = scatter_sum(row_sums.reshape(n_wide, own_rows), "wide", n_wide).reshape(own_rows)
    seeded = (seed_label[:, 0] < SEED_CLASSES).astype(jnp.float32)
    diag_column = (degree + SEED_WEIGHT * seeded + PRIOR)[:, None]

    def product(values):
        gathered = gather_blocks(values, "narrow", n_narrow).reshape(n_narrow * own_rows, width)
        rows = gather_blocks(values, "wide", n_wide)
        partial = jnp.dot(dense, gathered, precision=lax.Precision.HIGHEST)
        partial = partial.reshape(n_wide, own_rows, width)
        quad = jnp.zeros((width,), jnp.float32)
        for entry in range(n_wide):
            block = lax.dynamic_index_in_dim(
                partial, source("wide", n_wide, entry), 0, keepdims=False
            )
            quad = quad + jnp.sum(rows[entry] * block, axis=0)
        return scatter_sum(partial, "wide", n_wide), quad

    def reduce_dots(values):
        return sum_over(values, ("wide", "narrow"), n_all)

    labels = seed_label[:, 0]
    rhs = SEED_WEIGHT * (
        labels[:, None] == jnp.arange(SEED_CLASSES, dtype=jnp.int32)[None, :]
    ).astype(jnp.float32)
    solution = jnp.zeros_like(rhs)
    residual = rhs
    direction = rhs
    weighted, quad = product(direction)
    image = diag_column * direction - weighted
    first = reduce_dots(
        jnp.stack(
            [
                jnp.sum(residual * residual, axis=0),
                jnp.sum(diag_column * direction * direction, axis=0) - quad,
            ]
        )
    )
    norm_now = first[0]
    curvature = first[1]
    for step in range(ITERS):
        alpha = norm_now / curvature
        solution = solution + alpha * direction
        residual = residual - alpha * image
        if step == ITERS - 1:
            break
        weighted_residual, quad = product(residual)
        sums = reduce_dots(
            jnp.stack(
                [
                    jnp.sum(residual * residual, axis=0),
                    jnp.sum(diag_column * residual * residual, axis=0) - quad,
                    jnp.sum(residual * image, axis=0),
                    jnp.sum(direction * image, axis=0),
                ]
            )
        )
        norm_next = sums[0]
        ratio = norm_next / norm_now
        curvature = sums[1] + ratio * (2.0 * sums[2] + ratio * sums[3])
        direction = residual + ratio * direction
        weighted = weighted_residual + ratio * weighted
        image = diag_column * direction - weighted
        norm_now = norm_next
    return (solution, residual)


def solution(mesh):
    placed = (
        P(("vol", "narrow"), "wide", None, None),
        P(("vol", "narrow"), "wide"),
        P(("vol", "narrow", "wide"), None),
    )
    return jax.shard_map(
        local,
        mesh=mesh,
        in_specs=placed,
        out_specs=(P(("vol", "narrow", "wide"), None), P(("vol", "narrow", "wide"), None)),
        check_vma=False,
    )
```

```python
import jax
import jax.numpy as jnp
from jax import lax
from jax.sharding import PartitionSpec as P

SEED_CLASSES = 128
ITERS = 3


SEED_WEIGHT = 2.0
PRIOR = 0.5


def sum_over(values, axes, count):
    spread = jnp.broadcast_to(values[None], (count,) + values.shape)
    return jnp.sum(lax.all_to_all(spread, axes, 0, 0, tiled=True), axis=0)


def scatter_sum(blocks, axis, count):
    if count > 4:
        return jnp.sum(lax.all_to_all(blocks, axis, 0, 0, tiled=True), axis=0)
    me = lax.axis_index(axis)
    total = lax.dynamic_index_in_dim(blocks, me, 0, keepdims=False)
    for shift in range(1, count):
        sent = lax.dynamic_index_in_dim(blocks, (me + shift) % count, 0, keepdims=False)
        pairs = [(i, (i + shift) % count) for i in range(count)]
        total = total + lax.ppermute(sent, axis, pairs)
    return total


def gather_blocks(values, axis, count):
    if count > 4:
        return lax.all_gather(values, axis, axis=0, tiled=False)
    parts = [values]
    for shift in range(1, count):
        pairs = [(i, (i + shift) % count) for i in range(count)]
        parts.append(lax.ppermute(values, axis, pairs))
    return jnp.stack(parts)


def source(axis, count, entry):
    if count > 4:
        return entry
    return (lax.axis_index(axis) - entry) % count


def local(tiles, pattern, seed_label):
    groups = tiles.shape[0]
    tile = tiles.shape[2]
    own_rows = seed_label.shape[0]
    br_local = own_rows // tile
    n_wide = lax.axis_size("wide")
    n_narrow = lax.axis_size("narrow")
    n_all = n_wide * n_narrow
    width = SEED_CLASSES
    column_blocks = n_narrow * br_local
    local_column = pattern // groups * br_local + pattern % br_local
    pick = local_column[:, :, None] == jnp.arange(column_blocks, dtype=local_column.dtype)
    dense = jnp.sum(
        jnp.where(pick[:, :, None, :, None], tiles[:, :, :, None, :], 0.0), axis=1
    )
    column_sums = jnp.sum(dense, axis=(0, 1)).reshape(n_narrow, own_rows)
    degree = scatter_sum(column_sums, "narrow", n_narrow)
    order = source("wide", n_wide, jnp.arange(n_wide))
    dense = jnp.take(dense.reshape(n_wide, own_rows, column_blocks * tile), order, axis=0)
    transposed = dense.reshape(groups * tile, column_blocks * tile).T

    labels = seed_label[:, 0]
    seeded = (labels < SEED_CLASSES).astype(jnp.float32)
    diag_column = (degree + SEED_WEIGHT * seeded + PRIOR)[:, None]
    classes = jnp.arange(SEED_CLASSES, dtype=jnp.int32)

    def indicator(values):
        return SEED_WEIGHT * (values[..., None] == classes).astype(jnp.float32)

    def product(row_values, column_values):
        partial = jnp.dot(
            transposed, row_values.reshape(groups * tile, width), precision=lax.Precision.HIGHEST
        ).reshape(n_narrow, own_rows, width)
        quad = jnp.zeros((width,), jnp.float32)
        for entry in range(n_narrow):
            block = lax.dynamic_index_in_dim(
                partial, source("narrow", n_narrow, entry), 0, keepdims=False
            )
            quad = quad + jnp.sum(column_values[entry] * block, axis=0)
        return scatter_sum(partial, "narrow", n_narrow), quad

    def product_of(values):
        return product(
            gather_blocks(values, "wide", n_wide), gather_blocks(values, "narrow", n_narrow)
        )

    def reduce_dots(values):
        return sum_over(values, ("wide", "narrow"), n_all)

    rhs = indicator(labels)
    solution = jnp.zeros_like(rhs)
    residual = rhs
    direction = rhs
    weighted, quad = product(
        indicator(gather_blocks(labels, "wide", n_wide)),
        indicator(gather_blocks(labels, "narrow", n_narrow)),
    )
    image = diag_column * direction - weighted
    first = reduce_dots(
        jnp.stack(
            [
                jnp.sum(residual * residual, axis=0),
                jnp.sum(diag_column * direction * direction, axis=0) - quad,
            ]
        )
    )
    norm_now = first[0]
    curvature = first[1]
    for step in range(ITERS):
        alpha = norm_now / curvature
        solution = solution + alpha * direction
        residual = residual - alpha * image
        if step == ITERS - 1:
            break
        weighted_residual, quad = product_of(residual)
        sums = reduce_dots(
            jnp.stack(
                [
                    jnp.sum(residual * residual, axis=0),
                    jnp.sum(diag_column * residual * residual, axis=0) - quad,
                    jnp.sum(residual * image, axis=0),
                    jnp.sum(direction * image, axis=0),
                ]
            )
        )
        norm_next = sums[0]
        ratio = norm_next / norm_now
        curvature = sums[1] + ratio * (2.0 * sums[2] + ratio * sums[3])
        direction = residual + ratio * direction
        weighted = weighted_residual + ratio * weighted
        image = diag_column * direction - weighted
        norm_now = norm_next
    return (solution, residual)


def solution(mesh):
    placed = (
        P(("vol", "narrow"), "wide", None, None),
        P(("vol", "narrow"), "wide"),
        P(("vol", "narrow", "wide"), None),
    )
    return jax.shard_map(
        local,
        mesh=mesh,
        in_specs=placed,
        out_specs=(P(("vol", "narrow", "wide"), None), P(("vol", "narrow", "wide"), None)),
        check_vma=False,
    )
```

```python
import jax
import jax.numpy as jnp
from jax import lax
from jax.sharding import PartitionSpec as P

SEED_CLASSES = 128
ITERS = 3


SEED_WEIGHT = 2.0
PRIOR = 0.5


def sum_over(values, axes, count):
    spread = jnp.broadcast_to(values[None], (count,) + values.shape)
    return jnp.sum(lax.all_to_all(spread, axes, 0, 0, tiled=True), axis=0)


def scatter_sum(blocks, axis, count):
    if count > 4:
        return jnp.sum(lax.all_to_all(blocks, axis, 0, 0, tiled=True), axis=0)
    me = lax.axis_index(axis)
    total = lax.dynamic_index_in_dim(blocks, me, 0, keepdims=False)
    for shift in range(1, count):
        sent = lax.dynamic_index_in_dim(blocks, (me + shift) % count, 0, keepdims=False)
        pairs = [(i, (i + shift) % count) for i in range(count)]
        total = total + lax.ppermute(sent, axis, pairs)
    return total


def gather_blocks(values, axis, count):
    if count > 4:
        return lax.all_gather(values, axis, axis=0, tiled=False)
    parts = [values]
    for shift in range(1, count):
        pairs = [(i, (i + shift) % count) for i in range(count)]
        parts.append(lax.ppermute(values, axis, pairs))
    return jnp.stack(parts)


def source(axis, count, entry):
    if count > 4:
        return entry
    return (lax.axis_index(axis) - entry) % count


def local(tiles, pattern, seed_label):
    groups = tiles.shape[0]
    tile = tiles.shape[2]
    own_rows = seed_label.shape[0]
    br_local = own_rows // tile
    n_wide = lax.axis_size("wide")
    n_narrow = lax.axis_size("narrow")
    n_all = n_wide * n_narrow
    width = SEED_CLASSES
    column_blocks = n_narrow * br_local
    local_column = pattern // groups * br_local + pattern % br_local
    pick = local_column[:, :, None] == jnp.arange(column_blocks, dtype=local_column.dtype)
    dense = jnp.sum(
        jnp.where(pick[:, :, None, :, None], tiles[:, :, :, None, :], 0.0), axis=1
    )
    column_sums = jnp.sum(dense, axis=(0, 1)).reshape(n_narrow, own_rows)
    degree = scatter_sum(column_sums, "narrow", n_narrow)
    order = source("wide", n_wide, jnp.arange(n_wide))
    dense = jnp.take(dense.reshape(n_wide, own_rows, column_blocks * tile), order, axis=0)
    transposed = dense.reshape(groups * tile, column_blocks * tile).T

    labels = seed_label[:, 0]
    seeded = (labels < SEED_CLASSES).astype(jnp.float32)
    diag_column = (degree + SEED_WEIGHT * seeded + PRIOR)[:, None]
    classes = jnp.arange(SEED_CLASSES, dtype=jnp.int32)

    def indicator(values):
        return SEED_WEIGHT * (values[..., None] == classes).astype(jnp.float32)

    def product(row_values):
        partial = jnp.dot(
            transposed, row_values.reshape(groups * tile, width), precision=lax.Precision.HIGHEST
        ).reshape(n_narrow, own_rows, width)
        return scatter_sum(partial, "narrow", n_narrow)

    def reduce_dots(values):
        return sum_over(values, ("wide", "narrow"), n_all)

    rhs = indicator(labels)
    solution = jnp.zeros_like(rhs)
    residual = rhs
    direction = rhs
    rows_residual = indicator(gather_blocks(labels, "wide", n_wide))
    image = diag_column * direction - product(rows_residual)
    rows_image = gather_blocks(image, "wide", n_wide)
    first = reduce_dots(
        jnp.stack([jnp.sum(residual * residual, axis=0), jnp.sum(direction * image, axis=0)])
    )
    norm_now = first[0]
    curvature = first[1]
    for step in range(ITERS):
        alpha = norm_now / curvature
        solution = solution + alpha * direction
        residual = residual - alpha * image
        if step == ITERS - 1:
            break
        rows_residual = rows_residual - alpha * rows_image
        applied = diag_column * residual - product(rows_residual)
        rows_applied = gather_blocks(applied, "wide", n_wide)
        sums = reduce_dots(
            jnp.stack(
                [
                    jnp.sum(residual * residual, axis=0),
                    jnp.sum(residual * applied, axis=0),
                    jnp.sum(residual * image, axis=0),
                    jnp.sum(direction * image, axis=0),
                ]
            )
        )
        norm_next = sums[0]
        ratio = norm_next / norm_now
        curvature = sums[1] + ratio * (2.0 * sums[2] + ratio * sums[3])
        direction = residual + ratio * direction
        image = applied + ratio * image
        rows_image = rows_applied + ratio * rows_image
        norm_now = norm_next
    return (solution, residual)


def solution(mesh):
    placed = (
        P(("vol", "narrow"), "wide", None, None),
        P(("vol", "narrow"), "wide"),
        P(("vol", "narrow", "wide"), None),
    )
    return jax.shard_map(
        local,
        mesh=mesh,
        in_specs=placed,
        out_specs=(P(("vol", "narrow", "wide"), None), P(("vol", "narrow", "wide"), None)),
        check_vma=False,
    )
```

```python
import jax
import jax.numpy as jnp
from jax import lax
from jax.sharding import PartitionSpec as P

SEED_CLASSES = 128
ITERS = 3


SEED_WEIGHT = 2.0
PRIOR = 0.5


def sum_over(values, axes, count):
    spread = jnp.broadcast_to(values[None], (count,) + values.shape)
    return jnp.sum(lax.all_to_all(spread, axes, 0, 0, tiled=True), axis=0)


def scatter_sum(blocks, axis, count):
    if count > 4:
        return jnp.sum(lax.all_to_all(blocks, axis, 0, 0, tiled=True), axis=0)
    me = lax.axis_index(axis)
    total = lax.dynamic_index_in_dim(blocks, me, 0, keepdims=False)
    for shift in range(1, count):
        sent = lax.dynamic_index_in_dim(blocks, (me + shift) % count, 0, keepdims=False)
        pairs = [(i, (i + shift) % count) for i in range(count)]
        total = total + lax.ppermute(sent, axis, pairs)
    return total


def gather_blocks(values, axis, count):
    if count > 4:
        return lax.all_gather(values, axis, axis=0, tiled=False)
    parts = [values]
    for shift in range(1, count):
        pairs = [(i, (i + shift) % count) for i in range(count)]
        parts.append(lax.ppermute(values, axis, pairs))
    return jnp.stack(parts)


def scatter_with(blocks, extra, axis, count):
    rows = blocks.shape[1]
    if count > 4:
        payload = jnp.concatenate(
            [blocks, jnp.broadcast_to(extra[None], (count,) + extra.shape)], axis=1
        )
        got = lax.all_to_all(payload, axis, 0, 0, tiled=True)
        return jnp.sum(got[:, :rows], axis=0), got[:, rows:]
    me = lax.axis_index(axis)
    total = lax.dynamic_index_in_dim(blocks, me, 0, keepdims=False)
    extras = [extra]
    for shift in range(1, count):
        sent = lax.dynamic_index_in_dim(blocks, (me + shift) % count, 0, keepdims=False)
        pairs = [(i, (i + shift) % count) for i in range(count)]
        got = lax.ppermute(jnp.concatenate([sent, extra], axis=0), axis, pairs)
        total = total + got[:rows]
        extras.append(got[rows:])
    return total, jnp.stack(extras)


def canonical_sum(extras, axis, count):
    if count > 4:
        return jnp.sum(extras, axis=0)
    order = (lax.axis_index(axis) - jnp.arange(count)) % count
    return jnp.sum(jnp.take(extras, order, axis=0), axis=0)


def source(axis, count, entry):
    if count > 4:
        return entry
    return (lax.axis_index(axis) - entry) % count


def local(tiles, pattern, seed_label):
    groups = tiles.shape[0]
    tile = tiles.shape[2]
    own_rows = seed_label.shape[0]
    br_local = own_rows // tile
    n_wide = lax.axis_size("wide")
    n_narrow = lax.axis_size("narrow")
    n_all = n_wide * n_narrow
    width = SEED_CLASSES
    column_blocks = n_narrow * br_local
    local_column = pattern // groups * br_local + pattern % br_local
    pick = local_column[:, :, None] == jnp.arange(column_blocks, dtype=local_column.dtype)
    dense = jnp.sum(
        jnp.where(pick[:, :, None, :, None], tiles[:, :, :, None, :], 0.0), axis=1
    )
    column_sums = jnp.sum(dense, axis=(0, 1)).reshape(n_narrow, own_rows)
    degree = scatter_sum(column_sums, "narrow", n_narrow)
    order = source("wide", n_wide, jnp.arange(n_wide))
    dense = jnp.take(dense.reshape(n_wide, own_rows, column_blocks * tile), order, axis=0)
    transposed = dense.reshape(groups * tile, column_blocks * tile).T

    labels = seed_label[:, 0]
    seeded = (labels < SEED_CLASSES).astype(jnp.float32)
    diag_column = (degree + SEED_WEIGHT * seeded + PRIOR)[:, None]
    classes = jnp.arange(SEED_CLASSES, dtype=jnp.int32)

    def indicator(values):
        return SEED_WEIGHT * (values[..., None] == classes).astype(jnp.float32)

    def product(row_values, column_values):
        partial = jnp.dot(
            transposed, row_values.reshape(groups * tile, width), precision=lax.Precision.HIGHEST
        ).reshape(n_narrow, own_rows, width)
        quad = jnp.zeros((width,), jnp.float32)
        for entry in range(n_narrow):
            block = lax.dynamic_index_in_dim(
                partial, source("narrow", n_narrow, entry), 0, keepdims=False
            )
            quad = quad + jnp.sum(column_values[entry] * block, axis=0)
        return partial, quad

    def exchange(partial, partial_sums, applied_of, last):
        weighted, extras = scatter_with(partial, partial_sums, "narrow", n_narrow)
        narrow_sums = canonical_sum(extras, "narrow", n_narrow)
        applied = applied_of(weighted)
        if last:
            sums = canonical_sum(gather_blocks(narrow_sums, "wide", n_wide), "wide", n_wide)
            return applied, None, None, sums
        got = gather_blocks(jnp.concatenate([applied, narrow_sums], axis=0), "wide", n_wide)
        sums = canonical_sum(got[:, own_rows:], "wide", n_wide)
        return applied, got[:, :own_rows], gather_blocks(applied, "narrow", n_narrow), sums

    rhs = indicator(labels)
    solution = jnp.zeros_like(rhs)
    residual = rhs
    direction = rhs
    rows_residual = indicator(gather_blocks(labels, "wide", n_wide))
    columns_residual = indicator(gather_blocks(labels, "narrow", n_narrow))
    partial, quad = product(rows_residual, columns_residual)
    partial_sums = jnp.stack(
        [
            jnp.sum(residual * residual, axis=0),
            jnp.sum(diag_column * direction * direction, axis=0) - quad,
        ]
    )
    image, rows_image, columns_image, first = exchange(
        partial, partial_sums, lambda weighted: diag_column * direction - weighted, ITERS == 1
    )
    norm_now = first[0]
    curvature = first[1]
    for step in range(ITERS):
        alpha = norm_now / curvature
        solution = solution + alpha * direction
        residual = residual - alpha * image
        if step == ITERS - 1:
            break
        rows_residual = rows_residual - alpha * rows_image
        columns_residual = columns_residual - alpha * columns_image
        partial, quad = product(rows_residual, columns_residual)
        partial_sums = jnp.stack(
            [
                jnp.sum(residual * residual, axis=0),
                jnp.sum(diag_column * residual * residual, axis=0) - quad,
                jnp.sum(residual * image, axis=0),
                jnp.sum(direction * image, axis=0),
            ]
        )
        applied, rows_applied, columns_applied, sums = exchange(
            partial,
            partial_sums,
            lambda weighted: diag_column * residual - weighted,
            step == ITERS - 2,
        )
        norm_next = sums[0]
        ratio = norm_next / norm_now
        curvature = sums[1] + ratio * (2.0 * sums[2] + ratio * sums[3])
        direction = residual + ratio * direction
        image = applied + ratio * image
        if step < ITERS - 2:
            rows_image = rows_applied + ratio * rows_image
            columns_image = columns_applied + ratio * columns_image
        norm_now = norm_next
    return (solution, residual)


def solution(mesh):
    placed = (
        P(("vol", "narrow"), "wide", None, None),
        P(("vol", "narrow"), "wide"),
        P(("vol", "narrow", "wide"), None),
    )
    return jax.shard_map(
        local,
        mesh=mesh,
        in_specs=placed,
        out_specs=(P(("vol", "narrow", "wide"), None), P(("vol", "narrow", "wide"), None)),
        check_vma=False,
    )
```

```python
import jax
import jax.numpy as jnp
from jax import lax
from jax.sharding import PartitionSpec as P

SEED_CLASSES = 128
ITERS = 3


SEED_WEIGHT = 2.0
PRIOR = 0.5


def sum_over(values, axes, count):
    spread = jnp.broadcast_to(values[None], (count,) + values.shape)
    return jnp.sum(lax.all_to_all(spread, axes, 0, 0, tiled=True), axis=0)


def scatter_sum(blocks, axis, count):
    if count > 4:
        return jnp.sum(lax.all_to_all(blocks, axis, 0, 0, tiled=True), axis=0)
    me = lax.axis_index(axis)
    total = lax.dynamic_index_in_dim(blocks, me, 0, keepdims=False)
    for shift in range(1, count):
        sent = lax.dynamic_index_in_dim(blocks, (me + shift) % count, 0, keepdims=False)
        pairs = [(i, (i + shift) % count) for i in range(count)]
        total = total + lax.ppermute(sent, axis, pairs)
    return total


def gather_blocks(values, axis, count):
    if count > 4:
        return lax.all_gather(values, axis, axis=0, tiled=False)
    parts = [values]
    for shift in range(1, count):
        pairs = [(i, (i + shift) % count) for i in range(count)]
        parts.append(lax.ppermute(values, axis, pairs))
    return jnp.stack(parts)


def scatter_with(blocks, extra, axis, count):
    rows = blocks.shape[1]
    if count > 4:
        payload = jnp.concatenate(
            [blocks, jnp.broadcast_to(extra[None], (count,) + extra.shape)], axis=1
        )
        got = lax.all_to_all(payload, axis, 0, 0, tiled=True)
        return jnp.sum(got[:, :rows], axis=0), got[:, rows:]
    me = lax.axis_index(axis)
    total = lax.dynamic_index_in_dim(blocks, me, 0, keepdims=False)
    extras = [extra]
    for shift in range(1, count):
        sent = lax.dynamic_index_in_dim(blocks, (me + shift) % count, 0, keepdims=False)
        pairs = [(i, (i + shift) % count) for i in range(count)]
        got = lax.ppermute(jnp.concatenate([sent, extra], axis=0), axis, pairs)
        total = total + got[:rows]
        extras.append(got[rows:])
    return total, jnp.stack(extras)


def canonical_sum(extras, axis, count):
    if count > 4:
        return jnp.sum(extras, axis=0)
    me = lax.axis_index(axis)
    total = None
    for device in range(count):
        wanted = (me - device) % count
        term = extras[count - 1]
        for entry in range(count - 2, -1, -1):
            term = jnp.where(wanted == entry, extras[entry], term)
        total = term if total is None else total + term
    return total


def source(axis, count, entry):
    if count > 4:
        return entry
    return (lax.axis_index(axis) - entry) % count


def local(tiles, pattern, seed_label):
    groups = tiles.shape[0]
    tile = tiles.shape[2]
    own_rows = seed_label.shape[0]
    br_local = own_rows // tile
    n_wide = lax.axis_size("wide")
    n_narrow = lax.axis_size("narrow")
    n_all = n_wide * n_narrow
    width = SEED_CLASSES
    column_blocks = n_narrow * br_local
    local_column = pattern // groups * br_local + pattern % br_local
    pick = local_column[:, :, None] == jnp.arange(column_blocks, dtype=local_column.dtype)
    dense = jnp.sum(
        jnp.where(pick[:, :, None, :, None], tiles[:, :, :, None, :], 0.0), axis=1
    )
    column_sums = jnp.sum(dense, axis=(0, 1)).reshape(n_narrow, own_rows)
    order = source("wide", n_wide, jnp.arange(n_wide))
    dense = jnp.take(dense.reshape(n_wide, own_rows, column_blocks * tile), order, axis=0)
    transposed = dense.reshape(groups * tile, column_blocks * tile).T

    labels = seed_label[:, 0]
    seeded = (labels < SEED_CLASSES).astype(jnp.float32)
    fixed_column = (SEED_WEIGHT * seeded + PRIOR)[:, None]
    classes = jnp.arange(SEED_CLASSES, dtype=jnp.int32)

    def indicator(values):
        return SEED_WEIGHT * (values[..., None] == classes).astype(jnp.float32)

    def product(row_values, column_values):
        partial = jnp.dot(
            transposed, row_values.reshape(groups * tile, width), precision=lax.Precision.HIGHEST
        ).reshape(n_narrow, own_rows, width)
        quad = jnp.zeros((width,), jnp.float32)
        for entry in range(n_narrow):
            block = lax.dynamic_index_in_dim(
                partial, source("narrow", n_narrow, entry), 0, keepdims=False
            )
            quad = quad + jnp.sum(column_values[entry] * block, axis=0)
        return partial, quad

    def narrow_step(partial, partial_sums):
        weighted, extras = scatter_with(partial, partial_sums, "narrow", n_narrow)
        return weighted, canonical_sum(extras, "narrow", n_narrow)

    def wide_step(applied, narrow_sums, last):
        if last:
            sums = canonical_sum(gather_blocks(narrow_sums, "wide", n_wide), "wide", n_wide)
            return None, None, sums
        got = gather_blocks(jnp.concatenate([applied, narrow_sums], axis=0), "wide", n_wide)
        sums = canonical_sum(got[:, own_rows:], "wide", n_wide)
        return got[:, :own_rows], gather_blocks(applied, "narrow", n_narrow), sums

    rhs = indicator(labels)
    solution = jnp.zeros_like(rhs)
    residual = rhs
    direction = rhs
    rows_residual = indicator(gather_blocks(labels, "wide", n_wide))
    columns_residual = indicator(gather_blocks(labels, "narrow", n_narrow))
    partial, quad = product(rows_residual, columns_residual)
    degree_part = jnp.zeros((width,), jnp.float32)
    for entry in range(n_narrow):
        sums_block = lax.dynamic_index_in_dim(
            column_sums, source("narrow", n_narrow, entry), 0, keepdims=False
        )
        degree_part = degree_part + jnp.sum(
            sums_block[:, None] * columns_residual[entry] * columns_residual[entry], axis=0
        )
    partial_sums = jnp.stack(
        [
            jnp.sum(residual * residual, axis=0),
            degree_part + jnp.sum(fixed_column * direction * direction, axis=0) - quad,
        ]
    )
    carried = jnp.concatenate([partial, column_sums[:, None, :]], axis=1)
    weighted, narrow_sums = narrow_step(carried, partial_sums)
    diag_column = weighted[own_rows][:, None] + fixed_column
    image = diag_column * direction - weighted[:own_rows]
    rows_image, columns_image, first = wide_step(image, narrow_sums, ITERS == 1)
    norm_now = first[0]
    curvature = first[1]
    for step in range(ITERS):
        alpha = norm_now / curvature
        solution = solution + alpha * direction
        residual = residual - alpha * image
        if step == ITERS - 1:
            break
        rows_residual = rows_residual - alpha * rows_image
        columns_residual = columns_residual - alpha * columns_image
        partial, quad = product(rows_residual, columns_residual)
        partial_sums = jnp.stack(
            [
                jnp.sum(residual * residual, axis=0),
                jnp.sum(diag_column * residual * residual, axis=0) - quad,
                jnp.sum(residual * image, axis=0),
                jnp.sum(direction * image, axis=0),
            ]
        )
        weighted, narrow_sums = narrow_step(partial, partial_sums)
        applied = diag_column * residual - weighted
        rows_applied, columns_applied, sums = wide_step(applied, narrow_sums, step == ITERS - 2)
        norm_next = sums[0]
        ratio = norm_next / norm_now
        curvature = sums[1] + ratio * (2.0 * sums[2] + ratio * sums[3])
        direction = residual + ratio * direction
        image = applied + ratio * image
        if step < ITERS - 2:
            rows_image = rows_applied + ratio * rows_image
            columns_image = columns_applied + ratio * columns_image
        norm_now = norm_next
    return (solution, residual)


def solution(mesh):
    placed = (
        P(("vol", "narrow"), "wide", None, None),
        P(("vol", "narrow"), "wide"),
        P(("vol", "narrow", "wide"), None),
    )
    return jax.shard_map(
        local,
        mesh=mesh,
        in_specs=placed,
        out_specs=(P(("vol", "narrow", "wide"), None), P(("vol", "narrow", "wide"), None)),
        check_vma=False,
    )
```

```python
import jax
import jax.numpy as jnp
from jax import lax
from jax.sharding import PartitionSpec as P

SEED_CLASSES = 128
ITERS = 3


SEED_WEIGHT = 2.0
PRIOR = 0.5


def sum_over(values, axes, count):
    spread = jnp.broadcast_to(values[None], (count,) + values.shape)
    return jnp.sum(lax.all_to_all(spread, axes, 0, 0, tiled=True), axis=0)


def scatter_sum(blocks, axis, count):
    if count > 4:
        return jnp.sum(lax.all_to_all(blocks, axis, 0, 0, tiled=True), axis=0)
    me = lax.axis_index(axis)
    total = lax.dynamic_index_in_dim(blocks, me, 0, keepdims=False)
    for shift in range(1, count):
        sent = lax.dynamic_index_in_dim(blocks, (me + shift) % count, 0, keepdims=False)
        pairs = [(i, (i + shift) % count) for i in range(count)]
        total = total + lax.ppermute(sent, axis, pairs)
    return total


def gather_blocks(values, axis, count):
    if count > 4 or axis == "narrow":
        return lax.all_gather(values, axis, axis=0, tiled=False)
    parts = [values]
    for shift in range(1, count):
        pairs = [(i, (i + shift) % count) for i in range(count)]
        parts.append(lax.ppermute(values, axis, pairs))
    return jnp.stack(parts)


def scatter_with(blocks, extra, axis, count):
    rows = blocks.shape[1]
    if count > 4:
        payload = jnp.concatenate(
            [blocks, jnp.broadcast_to(extra[None], (count,) + extra.shape)], axis=1
        )
        got = lax.all_to_all(payload, axis, 0, 0, tiled=True)
        return jnp.sum(got[:, :rows], axis=0), got[:, rows:]
    me = lax.axis_index(axis)
    total = lax.dynamic_index_in_dim(blocks, me, 0, keepdims=False)
    extras = [extra]
    for shift in range(1, count):
        sent = lax.dynamic_index_in_dim(blocks, (me + shift) % count, 0, keepdims=False)
        pairs = [(i, (i + shift) % count) for i in range(count)]
        got = lax.ppermute(jnp.concatenate([sent, extra], axis=0), axis, pairs)
        total = total + got[:rows]
        extras.append(got[rows:])
    return total, jnp.stack(extras)


def canonical_sum(extras, axis, count):
    if count > 4:
        return jnp.sum(extras, axis=0)
    me = lax.axis_index(axis)
    total = None
    for device in range(count):
        wanted = (me - device) % count
        term = extras[count - 1]
        for entry in range(count - 2, -1, -1):
            term = jnp.where(wanted == entry, extras[entry], term)
        total = term if total is None else total + term
    return total


def source(axis, count, entry):
    if count > 4 or axis == "narrow":
        return entry
    return (lax.axis_index(axis) - entry) % count


def local(tiles, pattern, seed_label):
    groups = tiles.shape[0]
    tile = tiles.shape[2]
    own_rows = seed_label.shape[0]
    br_local = own_rows // tile
    n_wide = lax.axis_size("wide")
    n_narrow = lax.axis_size("narrow")
    n_all = n_wide * n_narrow
    width = SEED_CLASSES
    column_blocks = n_narrow * br_local
    local_column = pattern // groups * br_local + pattern % br_local
    pick = local_column[:, :, None] == jnp.arange(column_blocks, dtype=local_column.dtype)
    dense = jnp.sum(
        jnp.where(pick[:, :, None, :, None], tiles[:, :, :, None, :], 0.0), axis=1
    )
    column_sums = jnp.sum(dense, axis=(0, 1)).reshape(n_narrow, own_rows)
    order = source("wide", n_wide, jnp.arange(n_wide))
    dense = jnp.take(dense.reshape(n_wide, own_rows, column_blocks * tile), order, axis=0)
    transposed = dense.reshape(groups * tile, column_blocks * tile).T

    labels = seed_label[:, 0]
    seeded = (labels < SEED_CLASSES).astype(jnp.float32)
    fixed_column = (SEED_WEIGHT * seeded + PRIOR)[:, None]
    classes = jnp.arange(SEED_CLASSES, dtype=jnp.int32)

    def indicator(values):
        return SEED_WEIGHT * (values[..., None] == classes).astype(jnp.float32)

    def product(row_values, column_values):
        partial = jnp.dot(
            transposed, row_values.reshape(groups * tile, width), precision=lax.Precision.HIGHEST
        ).reshape(n_narrow, own_rows, width)
        quad = jnp.zeros((width,), jnp.float32)
        for entry in range(n_narrow):
            block = lax.dynamic_index_in_dim(
                partial, source("narrow", n_narrow, entry), 0, keepdims=False
            )
            quad = quad + jnp.sum(column_values[entry] * block, axis=0)
        return partial, quad

    def narrow_step(partial, partial_sums):
        weighted, extras = scatter_with(partial, partial_sums, "narrow", n_narrow)
        return weighted, canonical_sum(extras, "narrow", n_narrow)

    def wide_step(applied, narrow_sums, last):
        if last:
            sums = canonical_sum(gather_blocks(narrow_sums, "wide", n_wide), "wide", n_wide)
            return None, None, sums
        got = gather_blocks(jnp.concatenate([applied, narrow_sums], axis=0), "wide", n_wide)
        sums = canonical_sum(got[:, own_rows:], "wide", n_wide)
        return got[:, :own_rows], gather_blocks(applied, "narrow", n_narrow), sums

    rhs = indicator(labels)
    solution = jnp.zeros_like(rhs)
    residual = rhs
    direction = rhs
    rows_residual = indicator(gather_blocks(labels, "wide", n_wide))
    columns_residual = indicator(gather_blocks(labels, "narrow", n_narrow))
    partial, quad = product(rows_residual, columns_residual)
    degree_part = jnp.zeros((width,), jnp.float32)
    for entry in range(n_narrow):
        sums_block = lax.dynamic_index_in_dim(
            column_sums, source("narrow", n_narrow, entry), 0, keepdims=False
        )
        degree_part = degree_part + jnp.sum(
            sums_block[:, None] * columns_residual[entry] * columns_residual[entry], axis=0
        )
    partial_sums = jnp.stack(
        [
            jnp.sum(residual * residual, axis=0),
            degree_part + jnp.sum(fixed_column * direction * direction, axis=0) - quad,
        ]
    )
    carried = jnp.concatenate([partial, column_sums[:, None, :]], axis=1)
    weighted, narrow_sums = narrow_step(carried, partial_sums)
    diag_column = weighted[own_rows][:, None] + fixed_column
    image = diag_column * direction - weighted[:own_rows]
    rows_image, columns_image, first = wide_step(image, narrow_sums, ITERS == 1)
    norm_now = first[0]
    curvature = first[1]
    for step in range(ITERS):
        alpha = norm_now / curvature
        solution = solution + alpha * direction
        residual = residual - alpha * image
        if step == ITERS - 1:
            break
        rows_residual = rows_residual - alpha * rows_image
        columns_residual = columns_residual - alpha * columns_image
        partial, quad = product(rows_residual, columns_residual)
        partial_sums = jnp.stack(
            [
                jnp.sum(residual * residual, axis=0),
                jnp.sum(diag_column * residual * residual, axis=0) - quad,
                jnp.sum(residual * image, axis=0),
                jnp.sum(direction * image, axis=0),
            ]
        )
        weighted, narrow_sums = narrow_step(partial, partial_sums)
        applied = diag_column * residual - weighted
        rows_applied, columns_applied, sums = wide_step(applied, narrow_sums, step == ITERS - 2)
        norm_next = sums[0]
        ratio = norm_next / norm_now
        curvature = sums[1] + ratio * (2.0 * sums[2] + ratio * sums[3])
        direction = residual + ratio * direction
        image = applied + ratio * image
        if step < ITERS - 2:
            rows_image = rows_applied + ratio * rows_image
            columns_image = columns_applied + ratio * columns_image
        norm_now = norm_next
    return (solution, residual)


def solution(mesh):
    placed = (
        P(("vol", "narrow"), "wide", None, None),
        P(("vol", "narrow"), "wide"),
        P(("vol", "narrow", "wide"), None),
    )
    return jax.shard_map(
        local,
        mesh=mesh,
        in_specs=placed,
        out_specs=(P(("vol", "narrow", "wide"), None), P(("vol", "narrow", "wide"), None)),
        check_vma=False,
    )
```

```python
import jax
import jax.numpy as jnp
from jax import lax
from jax.sharding import PartitionSpec as P

SEED_CLASSES = 128
ITERS = 3


SEED_WEIGHT = 2.0
PRIOR = 0.5


def sum_over(values, axes, count):
    spread = jnp.broadcast_to(values[None], (count,) + values.shape)
    return jnp.sum(lax.all_to_all(spread, axes, 0, 0, tiled=True), axis=0)


def scatter_sum(blocks, axis, count):
    if count > 4:
        return jnp.sum(lax.all_to_all(blocks, axis, 0, 0, tiled=True), axis=0)
    me = lax.axis_index(axis)
    total = lax.dynamic_index_in_dim(blocks, me, 0, keepdims=False)
    for shift in range(1, count):
        sent = lax.dynamic_index_in_dim(blocks, (me + shift) % count, 0, keepdims=False)
        pairs = [(i, (i + shift) % count) for i in range(count)]
        total = total + lax.ppermute(sent, axis, pairs)
    return total


def gather_blocks(values, axis, count):
    if count > 4:
        return lax.all_gather(values, axis, axis=0, tiled=False)
    if axis == "narrow" and count == 4:
        partner = lax.ppermute(values, axis, [(i, i ^ 1) for i in range(count)])
        both = jnp.stack([values, partner])
        return jnp.concatenate([both, lax.ppermute(both, axis, [(i, i ^ 2) for i in range(count)])])
    parts = [values]
    for shift in range(1, count):
        pairs = [(i, (i + shift) % count) for i in range(count)]
        parts.append(lax.ppermute(values, axis, pairs))
    return jnp.stack(parts)


def scatter_with(blocks, extra, axis, count):
    rows = blocks.shape[1]
    if count > 4:
        payload = jnp.concatenate(
            [blocks, jnp.broadcast_to(extra[None], (count,) + extra.shape)], axis=1
        )
        got = lax.all_to_all(payload, axis, 0, 0, tiled=True)
        return jnp.sum(got[:, :rows], axis=0), got[:, rows:]
    me = lax.axis_index(axis)
    total = lax.dynamic_index_in_dim(blocks, me, 0, keepdims=False)
    extras = [extra]
    for shift in range(1, count):
        sent = lax.dynamic_index_in_dim(blocks, (me + shift) % count, 0, keepdims=False)
        pairs = [(i, (i + shift) % count) for i in range(count)]
        got = lax.ppermute(jnp.concatenate([sent, extra], axis=0), axis, pairs)
        total = total + got[:rows]
        extras.append(got[rows:])
    return total, jnp.stack(extras)


def canonical_sum(extras, axis, count):
    if count > 4:
        return jnp.sum(extras, axis=0)
    me = lax.axis_index(axis)
    total = None
    for device in range(count):
        wanted = (me - device) % count
        term = extras[count - 1]
        for entry in range(count - 2, -1, -1):
            term = jnp.where(wanted == entry, extras[entry], term)
        total = term if total is None else total + term
    return total


def source(axis, count, entry):
    if count > 4:
        return entry
    if axis == "narrow" and count == 4:
        return lax.axis_index(axis) ^ entry
    return (lax.axis_index(axis) - entry) % count


def local(tiles, pattern, seed_label):
    groups = tiles.shape[0]
    tile = tiles.shape[2]
    own_rows = seed_label.shape[0]
    br_local = own_rows // tile
    n_wide = lax.axis_size("wide")
    n_narrow = lax.axis_size("narrow")
    n_all = n_wide * n_narrow
    width = SEED_CLASSES
    column_blocks = n_narrow * br_local
    local_column = pattern // groups * br_local + pattern % br_local
    pick = local_column[:, :, None] == jnp.arange(column_blocks, dtype=local_column.dtype)
    dense = jnp.sum(
        jnp.where(pick[:, :, None, :, None], tiles[:, :, :, None, :], 0.0), axis=1
    )
    column_sums = jnp.sum(dense, axis=(0, 1)).reshape(n_narrow, own_rows)
    order = source("wide", n_wide, jnp.arange(n_wide))
    dense = jnp.take(dense.reshape(n_wide, own_rows, column_blocks * tile), order, axis=0)
    transposed = dense.reshape(groups * tile, column_blocks * tile).T

    labels = seed_label[:, 0]
    seeded = (labels < SEED_CLASSES).astype(jnp.float32)
    fixed_column = (SEED_WEIGHT * seeded + PRIOR)[:, None]
    classes = jnp.arange(SEED_CLASSES, dtype=jnp.int32)

    def indicator(values):
        return SEED_WEIGHT * (values[..., None] == classes).astype(jnp.float32)

    def product(row_values, column_values):
        partial = jnp.dot(
            transposed, row_values.reshape(groups * tile, width), precision=lax.Precision.HIGHEST
        ).reshape(n_narrow, own_rows, width)
        quad = jnp.zeros((width,), jnp.float32)
        for entry in range(n_narrow):
            block = lax.dynamic_index_in_dim(
                partial, source("narrow", n_narrow, entry), 0, keepdims=False
            )
            quad = quad + jnp.sum(column_values[entry] * block, axis=0)
        return partial, quad

    def narrow_step(partial, partial_sums):
        weighted, extras = scatter_with(partial, partial_sums, "narrow", n_narrow)
        return weighted, canonical_sum(extras, "narrow", n_narrow)

    def wide_step(applied, narrow_sums, last):
        if last:
            sums = canonical_sum(gather_blocks(narrow_sums, "wide", n_wide), "wide", n_wide)
            return None, None, sums
        got = gather_blocks(jnp.concatenate([applied, narrow_sums], axis=0), "wide", n_wide)
        sums = canonical_sum(got[:, own_rows:], "wide", n_wide)
        return got[:, :own_rows], gather_blocks(applied, "narrow", n_narrow), sums

    rhs = indicator(labels)
    solution = jnp.zeros_like(rhs)
    residual = rhs
    direction = rhs
    rows_residual = indicator(gather_blocks(labels, "wide", n_wide))
    columns_residual = indicator(gather_blocks(labels, "narrow", n_narrow))
    partial, quad = product(rows_residual, columns_residual)
    degree_part = jnp.zeros((width,), jnp.float32)
    for entry in range(n_narrow):
        sums_block = lax.dynamic_index_in_dim(
            column_sums, source("narrow", n_narrow, entry), 0, keepdims=False
        )
        degree_part = degree_part + jnp.sum(
            sums_block[:, None] * columns_residual[entry] * columns_residual[entry], axis=0
        )
    partial_sums = jnp.stack(
        [
            jnp.sum(residual * residual, axis=0),
            degree_part + jnp.sum(fixed_column * direction * direction, axis=0) - quad,
        ]
    )
    carried = jnp.concatenate([partial, column_sums[:, None, :]], axis=1)
    weighted, narrow_sums = narrow_step(carried, partial_sums)
    diag_column = weighted[own_rows][:, None] + fixed_column
    image = diag_column * direction - weighted[:own_rows]
    rows_image, columns_image, first = wide_step(image, narrow_sums, ITERS == 1)
    norm_now = first[0]
    curvature = first[1]
    for step in range(ITERS):
        alpha = norm_now / curvature
        solution = solution + alpha * direction
        residual = residual - alpha * image
        if step == ITERS - 1:
            break
        rows_residual = rows_residual - alpha * rows_image
        columns_residual = columns_residual - alpha * columns_image
        partial, quad = product(rows_residual, columns_residual)
        partial_sums = jnp.stack(
            [
                jnp.sum(residual * residual, axis=0),
                jnp.sum(diag_column * residual * residual, axis=0) - quad,
                jnp.sum(residual * image, axis=0),
                jnp.sum(direction * image, axis=0),
            ]
        )
        weighted, narrow_sums = narrow_step(partial, partial_sums)
        applied = diag_column * residual - weighted
        rows_applied, columns_applied, sums = wide_step(applied, narrow_sums, step == ITERS - 2)
        norm_next = sums[0]
        ratio = norm_next / norm_now
        curvature = sums[1] + ratio * (2.0 * sums[2] + ratio * sums[3])
        direction = residual + ratio * direction
        image = applied + ratio * image
        if step < ITERS - 2:
            rows_image = rows_applied + ratio * rows_image
            columns_image = columns_applied + ratio * columns_image
        norm_now = norm_next
    return (solution, residual)


def solution(mesh):
    placed = (
        P(("vol", "narrow"), "wide", None, None),
        P(("vol", "narrow"), "wide"),
        P(("vol", "narrow", "wide"), None),
    )
    return jax.shard_map(
        local,
        mesh=mesh,
        in_specs=placed,
        out_specs=(P(("vol", "narrow", "wide"), None), P(("vol", "narrow", "wide"), None)),
        check_vma=False,
    )
```

```python
import jax
import jax.numpy as jnp
from jax import lax
from jax.sharding import PartitionSpec as P

SEED_CLASSES = 128
ITERS = 3


SEED_WEIGHT = 2.0
PRIOR = 0.5


def sum_over(values, axes, count):
    spread = jnp.broadcast_to(values[None], (count,) + values.shape)
    return jnp.sum(lax.all_to_all(spread, axes, 0, 0, tiled=True), axis=0)


def scatter_sum(blocks, axis, count):
    if count > 4:
        return jnp.sum(lax.all_to_all(blocks, axis, 0, 0, tiled=True), axis=0)
    me = lax.axis_index(axis)
    total = lax.dynamic_index_in_dim(blocks, me, 0, keepdims=False)
    for shift in range(1, count):
        sent = lax.dynamic_index_in_dim(blocks, (me + shift) % count, 0, keepdims=False)
        pairs = [(i, (i + shift) % count) for i in range(count)]
        total = total + lax.ppermute(sent, axis, pairs)
    return total


def gather_blocks(values, axis, count):
    if count > 4:
        return lax.all_gather(values, axis, axis=0, tiled=False)
    if count == 4:
        partner = lax.ppermute(values, axis, [(i, i ^ 1) for i in range(count)])
        both = jnp.stack([values, partner])
        return jnp.concatenate([both, lax.ppermute(both, axis, [(i, i ^ 2) for i in range(count)])])
    parts = [values]
    for shift in range(1, count):
        pairs = [(i, (i + shift) % count) for i in range(count)]
        parts.append(lax.ppermute(values, axis, pairs))
    return jnp.stack(parts)


def scatter_with(blocks, extra, axis, count):
    rows = blocks.shape[1]
    if count > 4:
        payload = jnp.concatenate(
            [blocks, jnp.broadcast_to(extra[None], (count,) + extra.shape)], axis=1
        )
        got = lax.all_to_all(payload, axis, 0, 0, tiled=True)
        return jnp.sum(got[:, :rows], axis=0), got[:, rows:]
    me = lax.axis_index(axis)
    total = lax.dynamic_index_in_dim(blocks, me, 0, keepdims=False)
    extras = [extra]
    for shift in range(1, count):
        sent = lax.dynamic_index_in_dim(blocks, (me + shift) % count, 0, keepdims=False)
        pairs = [(i, (i + shift) % count) for i in range(count)]
        got = lax.ppermute(jnp.concatenate([sent, extra], axis=0), axis, pairs)
        total = total + got[:rows]
        extras.append(got[rows:])
    return total, jnp.stack(extras)


def canonical_sum(extras, axis, count, shifted):
    if count > 4:
        return jnp.sum(extras, axis=0)
    me = lax.axis_index(axis)
    total = None
    for device in range(count):
        wanted = (me - device) % count if shifted else source(axis, count, device)
        term = extras[count - 1]
        for entry in range(count - 2, -1, -1):
            term = jnp.where(wanted == entry, extras[entry], term)
        total = term if total is None else total + term
    return total


def source(axis, count, entry):
    if count > 4:
        return entry
    if count == 4:
        return lax.axis_index(axis) ^ entry
    return (lax.axis_index(axis) - entry) % count


def local(tiles, pattern, seed_label):
    groups = tiles.shape[0]
    tile = tiles.shape[2]
    own_rows = seed_label.shape[0]
    br_local = own_rows // tile
    n_wide = lax.axis_size("wide")
    n_narrow = lax.axis_size("narrow")
    n_all = n_wide * n_narrow
    width = SEED_CLASSES
    column_blocks = n_narrow * br_local
    local_column = pattern // groups * br_local + pattern % br_local
    pick = local_column[:, :, None] == jnp.arange(column_blocks, dtype=local_column.dtype)
    dense = jnp.sum(
        jnp.where(pick[:, :, None, :, None], tiles[:, :, :, None, :], 0.0), axis=1
    )
    column_sums = jnp.sum(dense, axis=(0, 1)).reshape(n_narrow, own_rows)
    order = source("wide", n_wide, jnp.arange(n_wide))
    dense = jnp.take(dense.reshape(n_wide, own_rows, column_blocks * tile), order, axis=0)
    transposed = dense.reshape(groups * tile, column_blocks * tile).T

    labels = seed_label[:, 0]
    seeded = (labels < SEED_CLASSES).astype(jnp.float32)
    fixed_column = (SEED_WEIGHT * seeded + PRIOR)[:, None]
    classes = jnp.arange(SEED_CLASSES, dtype=jnp.int32)

    def indicator(values):
        return SEED_WEIGHT * (values[..., None] == classes).astype(jnp.float32)

    def product(row_values, column_values):
        partial = jnp.dot(
            transposed, row_values.reshape(groups * tile, width), precision=lax.Precision.HIGHEST
        ).reshape(n_narrow, own_rows, width)
        quad = jnp.zeros((width,), jnp.float32)
        for entry in range(n_narrow):
            block = lax.dynamic_index_in_dim(
                partial, source("narrow", n_narrow, entry), 0, keepdims=False
            )
            quad = quad + jnp.sum(column_values[entry] * block, axis=0)
        return partial, quad

    def narrow_step(partial, partial_sums):
        weighted, extras = scatter_with(partial, partial_sums, "narrow", n_narrow)
        return weighted, canonical_sum(extras, "narrow", n_narrow, True)

    def wide_step(applied, narrow_sums, last):
        if last:
            sums = canonical_sum(gather_blocks(narrow_sums, "wide", n_wide), "wide", n_wide, False)
            return None, None, sums
        got = gather_blocks(jnp.concatenate([applied, narrow_sums], axis=0), "wide", n_wide)
        sums = canonical_sum(got[:, own_rows:], "wide", n_wide, False)
        return got[:, :own_rows], gather_blocks(applied, "narrow", n_narrow), sums

    rhs = indicator(labels)
    solution = jnp.zeros_like(rhs)
    residual = rhs
    direction = rhs
    rows_residual = indicator(gather_blocks(labels, "wide", n_wide))
    columns_residual = indicator(gather_blocks(labels, "narrow", n_narrow))
    partial, quad = product(rows_residual, columns_residual)
    degree_part = jnp.zeros((width,), jnp.float32)
    for entry in range(n_narrow):
        sums_block = lax.dynamic_index_in_dim(
            column_sums, source("narrow", n_narrow, entry), 0, keepdims=False
        )
        degree_part = degree_part + jnp.sum(
            sums_block[:, None] * columns_residual[entry] * columns_residual[entry], axis=0
        )
    partial_sums = jnp.stack(
        [
            jnp.sum(residual * residual, axis=0),
            degree_part + jnp.sum(fixed_column * direction * direction, axis=0) - quad,
        ]
    )
    carried = jnp.concatenate([partial, column_sums[:, None, :]], axis=1)
    weighted, narrow_sums = narrow_step(carried, partial_sums)
    diag_column = weighted[own_rows][:, None] + fixed_column
    image = diag_column * direction - weighted[:own_rows]
    rows_image, columns_image, first = wide_step(image, narrow_sums, ITERS == 1)
    norm_now = first[0]
    curvature = first[1]
    for step in range(ITERS):
        alpha = norm_now / curvature
        solution = solution + alpha * direction
        residual = residual - alpha * image
        if step == ITERS - 1:
            break
        rows_residual = rows_residual - alpha * rows_image
        columns_residual = columns_residual - alpha * columns_image
        partial, quad = product(rows_residual, columns_residual)
        partial_sums = jnp.stack(
            [
                jnp.sum(residual * residual, axis=0),
                jnp.sum(diag_column * residual * residual, axis=0) - quad,
                jnp.sum(residual * image, axis=0),
                jnp.sum(direction * image, axis=0),
            ]
        )
        weighted, narrow_sums = narrow_step(partial, partial_sums)
        applied = diag_column * residual - weighted
        rows_applied, columns_applied, sums = wide_step(applied, narrow_sums, step == ITERS - 2)
        norm_next = sums[0]
        ratio = norm_next / norm_now
        curvature = sums[1] + ratio * (2.0 * sums[2] + ratio * sums[3])
        direction = residual + ratio * direction
        image = applied + ratio * image
        if step < ITERS - 2:
            rows_image = rows_applied + ratio * rows_image
            columns_image = columns_applied + ratio * columns_image
        norm_now = norm_next
    return (solution, residual)


def solution(mesh):
    placed = (
        P(("vol", "narrow"), "wide", None, None),
        P(("vol", "narrow"), "wide"),
        P(("vol", "narrow", "wide"), None),
    )
    return jax.shard_map(
        local,
        mesh=mesh,
        in_specs=placed,
        out_specs=(P(("vol", "narrow", "wide"), None), P(("vol", "narrow", "wide"), None)),
        check_vma=False,
    )
```

```python
import jax
import jax.numpy as jnp
from jax import lax
from jax.sharding import PartitionSpec as P

SEED_CLASSES = 128
ITERS = 3


SEED_WEIGHT = 2.0
PRIOR = 0.5


def sum_over(values, axes, count):
    spread = jnp.broadcast_to(values[None], (count,) + values.shape)
    return jnp.sum(lax.all_to_all(spread, axes, 0, 0, tiled=True), axis=0)


def scatter_sum(blocks, axis, count):
    if count > 4:
        return jnp.sum(lax.all_to_all(blocks, axis, 0, 0, tiled=True), axis=0)
    me = lax.axis_index(axis)
    total = lax.dynamic_index_in_dim(blocks, me, 0, keepdims=False)
    for shift in range(1, count):
        sent = lax.dynamic_index_in_dim(blocks, (me + shift) % count, 0, keepdims=False)
        pairs = [(i, (i + shift) % count) for i in range(count)]
        total = total + lax.ppermute(sent, axis, pairs)
    return total


def gather_blocks(values, axis, count):
    if count > 4:
        return lax.all_gather(values, axis, axis=0, tiled=False)
    if axis == "narrow" and count == 4:
        partner = lax.ppermute(values, axis, [(i, i ^ 1) for i in range(count)])
        both = jnp.stack([values, partner])
        return jnp.concatenate([both, lax.ppermute(both, axis, [(i, i ^ 2) for i in range(count)])])
    parts = [values]
    for shift in range(1, count):
        pairs = [(i, (i + shift) % count) for i in range(count)]
        parts.append(lax.ppermute(values, axis, pairs))
    return jnp.stack(parts)


def scatter_with(blocks, extra, axis, count):
    rows = blocks.shape[1]
    if count > 4:
        payload = jnp.concatenate(
            [blocks, jnp.broadcast_to(extra[None], (count,) + extra.shape)], axis=1
        )
        got = lax.all_to_all(payload, axis, 0, 0, tiled=True)
        return jnp.sum(got[:, :rows], axis=0), got[:, rows:]
    me = lax.axis_index(axis)
    total = lax.dynamic_index_in_dim(blocks, me, 0, keepdims=False)
    extras = [extra]
    for shift in range(1, count):
        sent = lax.dynamic_index_in_dim(blocks, (me + shift) % count, 0, keepdims=False)
        pairs = [(i, (i + shift) % count) for i in range(count)]
        got = lax.ppermute(jnp.concatenate([sent, extra], axis=0), axis, pairs)
        total = total + got[:rows]
        extras.append(got[rows:])
    return total, jnp.stack(extras)


def natural(blocks, axis, count):
    if count > 4:
        return blocks
    me = lax.axis_index(axis)
    ordered = []
    for device in range(count):
        wanted = (me - device) % count
        block = blocks[count - 1]
        for entry in range(count - 2, -1, -1):
            block = jnp.where(wanted == entry, blocks[entry], block)
        ordered.append(block)
    return jnp.stack(ordered)


def canonical_sum(extras, axis, count):
    if count > 4:
        return jnp.sum(extras, axis=0)
    me = lax.axis_index(axis)
    total = None
    for device in range(count):
        wanted = (me - device) % count
        term = extras[count - 1]
        for entry in range(count - 2, -1, -1):
            term = jnp.where(wanted == entry, extras[entry], term)
        total = term if total is None else total + term
    return total


def source(axis, count, entry):
    if count > 4:
        return entry
    if axis == "narrow" and count == 4:
        return lax.axis_index(axis) ^ entry
    return (lax.axis_index(axis) - entry) % count


def local(tiles, pattern, seed_label):
    groups = tiles.shape[0]
    tile = tiles.shape[2]
    own_rows = seed_label.shape[0]
    br_local = own_rows // tile
    n_wide = lax.axis_size("wide")
    n_narrow = lax.axis_size("narrow")
    n_all = n_wide * n_narrow
    width = SEED_CLASSES
    column_blocks = n_narrow * br_local
    local_column = pattern // groups * br_local + pattern % br_local
    pick = (
        local_column[:, :, None] == jnp.arange(column_blocks, dtype=local_column.dtype)
    ).astype(jnp.float32)
    transposed = jnp.einsum("mkt,mkab->tbma", pick, tiles, precision=lax.Precision.HIGHEST)
    column_sums = jnp.sum(transposed, axis=(2, 3)).reshape(n_narrow, own_rows)
    transposed = transposed.reshape(column_blocks * tile, groups * tile)

    labels = seed_label[:, 0]
    seeded = (labels < SEED_CLASSES).astype(jnp.float32)
    fixed_column = (SEED_WEIGHT * seeded + PRIOR)[:, None]
    classes = jnp.arange(SEED_CLASSES, dtype=jnp.int32)

    def indicator(values):
        return SEED_WEIGHT * (values[..., None] == classes).astype(jnp.float32)

    def product(row_values, column_values):
        partial = jnp.dot(
            transposed, row_values.reshape(groups * tile, width), precision=lax.Precision.HIGHEST
        ).reshape(n_narrow, own_rows, width)
        quad = jnp.zeros((width,), jnp.float32)
        for entry in range(n_narrow):
            block = lax.dynamic_index_in_dim(
                partial, source("narrow", n_narrow, entry), 0, keepdims=False
            )
            quad = quad + jnp.sum(column_values[entry] * block, axis=0)
        return partial, quad

    def narrow_step(partial, partial_sums):
        weighted, extras = scatter_with(partial, partial_sums, "narrow", n_narrow)
        return weighted, canonical_sum(extras, "narrow", n_narrow)

    def wide_step(applied, narrow_sums, last):
        if last:
            sums = canonical_sum(gather_blocks(narrow_sums, "wide", n_wide), "wide", n_wide)
            return None, None, sums
        got = gather_blocks(jnp.concatenate([applied, narrow_sums], axis=0), "wide", n_wide)
        sums = canonical_sum(got[:, own_rows:], "wide", n_wide)
        rows = natural(got[:, :own_rows], "wide", n_wide)
        return rows, gather_blocks(applied, "narrow", n_narrow), sums

    rhs = indicator(labels)
    solution = jnp.zeros_like(rhs)
    residual = rhs
    direction = rhs
    rows_residual = indicator(natural(gather_blocks(labels, "wide", n_wide), "wide", n_wide))
    columns_residual = indicator(gather_blocks(labels, "narrow", n_narrow))
    partial, quad = product(rows_residual, columns_residual)
    degree_part = jnp.zeros((width,), jnp.float32)
    for entry in range(n_narrow):
        sums_block = lax.dynamic_index_in_dim(
            column_sums, source("narrow", n_narrow, entry), 0, keepdims=False
        )
        degree_part = degree_part + jnp.sum(
            sums_block[:, None] * columns_residual[entry] * columns_residual[entry], axis=0
        )
    partial_sums = jnp.stack(
        [
            jnp.sum(residual * residual, axis=0),
            degree_part + jnp.sum(fixed_column * direction * direction, axis=0) - quad,
        ]
    )
    carried = jnp.concatenate([partial, column_sums[:, None, :]], axis=1)
    weighted, narrow_sums = narrow_step(carried, partial_sums)
    diag_column = weighted[own_rows][:, None] + fixed_column
    image = diag_column * direction - weighted[:own_rows]
    rows_image, columns_image, first = wide_step(image, narrow_sums, ITERS == 1)
    norm_now = first[0]
    curvature = first[1]
    for step in range(ITERS):
        alpha = norm_now / curvature
        solution = solution + alpha * direction
        residual = residual - alpha * image
        if step == ITERS - 1:
            break
        rows_residual = rows_residual - alpha * rows_image
        columns_residual = columns_residual - alpha * columns_image
        partial, quad = product(rows_residual, columns_residual)
        partial_sums = jnp.stack(
            [
                jnp.sum(residual * residual, axis=0),
                jnp.sum(diag_column * residual * residual, axis=0) - quad,
                jnp.sum(residual * image, axis=0),
                jnp.sum(direction * image, axis=0),
            ]
        )
        weighted, narrow_sums = narrow_step(partial, partial_sums)
        applied = diag_column * residual - weighted
        rows_applied, columns_applied, sums = wide_step(applied, narrow_sums, step == ITERS - 2)
        norm_next = sums[0]
        ratio = norm_next / norm_now
        curvature = sums[1] + ratio * (2.0 * sums[2] + ratio * sums[3])
        direction = residual + ratio * direction
        image = applied + ratio * image
        if step < ITERS - 2:
            rows_image = rows_applied + ratio * rows_image
            columns_image = columns_applied + ratio * columns_image
        norm_now = norm_next
    return (solution, residual)


def solution(mesh):
    placed = (
        P(("vol", "narrow"), "wide", None, None),
        P(("vol", "narrow"), "wide"),
        P(("vol", "narrow", "wide"), None),
    )
    return jax.shard_map(
        local,
        mesh=mesh,
        in_specs=placed,
        out_specs=(P(("vol", "narrow", "wide"), None), P(("vol", "narrow", "wide"), None)),
        check_vma=False,
    )
```

```python
import jax
import jax.numpy as jnp
from jax import lax
from jax.sharding import PartitionSpec as P

SEED_CLASSES = 128
ITERS = 3


SEED_WEIGHT = 2.0
PRIOR = 0.5


def sum_over(values, axes, count):
    spread = jnp.broadcast_to(values[None], (count,) + values.shape)
    return jnp.sum(lax.all_to_all(spread, axes, 0, 0, tiled=True), axis=0)


def scatter_sum(blocks, axis, count):
    if count > 4:
        return jnp.sum(lax.all_to_all(blocks, axis, 0, 0, tiled=True), axis=0)
    me = lax.axis_index(axis)
    total = lax.dynamic_index_in_dim(blocks, me, 0, keepdims=False)
    for shift in range(1, count):
        sent = lax.dynamic_index_in_dim(blocks, (me + shift) % count, 0, keepdims=False)
        pairs = [(i, (i + shift) % count) for i in range(count)]
        total = total + lax.ppermute(sent, axis, pairs)
    return total


def gather_blocks(values, axis, count):
    if count > 4:
        return lax.all_gather(values, axis, axis=0, tiled=False)
    if axis == "narrow" and count == 4:
        partner = lax.ppermute(values, axis, [(i, i ^ 1) for i in range(count)])
        both = jnp.stack([values, partner])
        return jnp.concatenate([both, lax.ppermute(both, axis, [(i, i ^ 2) for i in range(count)])])
    parts = [values]
    for shift in range(1, count):
        pairs = [(i, (i + shift) % count) for i in range(count)]
        parts.append(lax.ppermute(values, axis, pairs))
    return jnp.stack(parts)


def scatter_with(blocks, extra, axis, count):
    rows = blocks.shape[1]
    if count == 4:
        me = lax.axis_index(axis)
        far = jnp.stack(
            [lax.dynamic_index_in_dim(blocks, me ^ 2, 0, keepdims=False),
             lax.dynamic_index_in_dim(blocks, me ^ 3, 0, keepdims=False)]
        )
        near = jnp.stack(
            [lax.dynamic_index_in_dim(blocks, me, 0, keepdims=False),
             lax.dynamic_index_in_dim(blocks, me ^ 1, 0, keepdims=False)]
        )
        sent = jnp.concatenate([far, jnp.broadcast_to(extra[None], (2,) + extra.shape)], axis=1)
        got = lax.ppermute(sent, axis, [(i, i ^ 2) for i in range(count)])
        near = near + got[:, :rows]
        pair = extra + got[0, rows:]
        got = lax.ppermute(
            jnp.concatenate([near[1], pair], axis=0), axis, [(i, i ^ 1) for i in range(count)]
        )
        return near[0] + got[:rows], pair + got[rows:]
    if count > 4:
        payload = jnp.concatenate(
            [blocks, jnp.broadcast_to(extra[None], (count,) + extra.shape)], axis=1
        )
        got = lax.all_to_all(payload, axis, 0, 0, tiled=True)
        return jnp.sum(got[:, :rows], axis=0), got[:, rows:]
    me = lax.axis_index(axis)
    total = lax.dynamic_index_in_dim(blocks, me, 0, keepdims=False)
    extras = [extra]
    for shift in range(1, count):
        sent = lax.dynamic_index_in_dim(blocks, (me + shift) % count, 0, keepdims=False)
        pairs = [(i, (i + shift) % count) for i in range(count)]
        got = lax.ppermute(jnp.concatenate([sent, extra], axis=0), axis, pairs)
        total = total + got[:rows]
        extras.append(got[rows:])
    return total, jnp.stack(extras)


def canonical_sum(extras, axis, count):
    if count > 4:
        return jnp.sum(extras, axis=0)
    me = lax.axis_index(axis)
    total = None
    for device in range(count):
        wanted = (me - device) % count
        term = extras[count - 1]
        for entry in range(count - 2, -1, -1):
            term = jnp.where(wanted == entry, extras[entry], term)
        total = term if total is None else total + term
    return total


def source(axis, count, entry):
    if count > 4:
        return entry
    if axis == "narrow" and count == 4:
        return lax.axis_index(axis) ^ entry
    return (lax.axis_index(axis) - entry) % count


def local(tiles, pattern, seed_label):
    groups = tiles.shape[0]
    tile = tiles.shape[2]
    own_rows = seed_label.shape[0]
    br_local = own_rows // tile
    n_wide = lax.axis_size("wide")
    n_narrow = lax.axis_size("narrow")
    n_all = n_wide * n_narrow
    width = SEED_CLASSES
    column_blocks = n_narrow * br_local
    local_column = pattern // groups * br_local + pattern % br_local
    pick = local_column[:, :, None] == jnp.arange(column_blocks, dtype=local_column.dtype)
    dense = jnp.sum(
        jnp.where(pick[:, :, None, :, None], tiles[:, :, :, None, :], 0.0), axis=1
    )
    column_sums = jnp.sum(dense, axis=(0, 1)).reshape(n_narrow, own_rows)
    order = source("wide", n_wide, jnp.arange(n_wide))
    dense = jnp.take(dense.reshape(n_wide, own_rows, column_blocks * tile), order, axis=0)
    transposed = dense.reshape(groups * tile, column_blocks * tile).T

    labels = seed_label[:, 0]
    seeded = (labels < SEED_CLASSES).astype(jnp.float32)
    fixed_column = (SEED_WEIGHT * seeded + PRIOR)[:, None]
    classes = jnp.arange(SEED_CLASSES, dtype=jnp.int32)

    def indicator(values):
        return SEED_WEIGHT * (values[..., None] == classes).astype(jnp.float32)

    def product(row_values, column_values):
        partial = jnp.dot(
            transposed, row_values.reshape(groups * tile, width), precision=lax.Precision.HIGHEST
        ).reshape(n_narrow, own_rows, width)
        quad = jnp.zeros((width,), jnp.float32)
        for entry in range(n_narrow):
            block = lax.dynamic_index_in_dim(
                partial, source("narrow", n_narrow, entry), 0, keepdims=False
            )
            quad = quad + jnp.sum(column_values[entry] * block, axis=0)
        return partial, quad

    def narrow_step(partial, partial_sums):
        weighted, extras = scatter_with(partial, partial_sums, "narrow", n_narrow)
        if n_narrow == 4:
            return weighted, extras
        return weighted, canonical_sum(extras, "narrow", n_narrow)

    def wide_step(applied, narrow_sums, last):
        if last:
            sums = canonical_sum(gather_blocks(narrow_sums, "wide", n_wide), "wide", n_wide)
            return None, None, sums
        got = gather_blocks(jnp.concatenate([applied, narrow_sums], axis=0), "wide", n_wide)
        sums = canonical_sum(got[:, own_rows:], "wide", n_wide)
        return got[:, :own_rows], gather_blocks(applied, "narrow", n_narrow), sums

    rhs = indicator(labels)
    solution = jnp.zeros_like(rhs)
    residual = rhs
    direction = rhs
    rows_residual = indicator(gather_blocks(labels, "wide", n_wide))
    columns_residual = indicator(gather_blocks(labels, "narrow", n_narrow))
    partial, quad = product(rows_residual, columns_residual)
    degree_part = jnp.zeros((width,), jnp.float32)
    for entry in range(n_narrow):
        sums_block = lax.dynamic_index_in_dim(
            column_sums, source("narrow", n_narrow, entry), 0, keepdims=False
        )
        degree_part = degree_part + jnp.sum(
            sums_block[:, None] * columns_residual[entry] * columns_residual[entry], axis=0
        )
    partial_sums = jnp.stack(
        [
            jnp.sum(residual * residual, axis=0),
            degree_part + jnp.sum(fixed_column * direction * direction, axis=0) - quad,
        ]
    )
    carried = jnp.concatenate([partial, column_sums[:, None, :]], axis=1)
    weighted, narrow_sums = narrow_step(carried, partial_sums)
    diag_column = weighted[own_rows][:, None] + fixed_column
    image = diag_column * direction - weighted[:own_rows]
    rows_image, columns_image, first = wide_step(image, narrow_sums, ITERS == 1)
    norm_now = first[0]
    curvature = first[1]
    for step in range(ITERS):
        alpha = norm_now / curvature
        solution = solution + alpha * direction
        residual = residual - alpha * image
        if step == ITERS - 1:
            break
        rows_residual = rows_residual - alpha * rows_image
        columns_residual = columns_residual - alpha * columns_image
        partial, quad = product(rows_residual, columns_residual)
        partial_sums = jnp.stack(
            [
                jnp.sum(residual * residual, axis=0),
                jnp.sum(diag_column * residual * residual, axis=0) - quad,
                jnp.sum(residual * image, axis=0),
                jnp.sum(direction * image, axis=0),
            ]
        )
        weighted, narrow_sums = narrow_step(partial, partial_sums)
        applied = diag_column * residual - weighted
        rows_applied, columns_applied, sums = wide_step(applied, narrow_sums, step == ITERS - 2)
        norm_next = sums[0]
        ratio = norm_next / norm_now
        curvature = sums[1] + ratio * (2.0 * sums[2] + ratio * sums[3])
        direction = residual + ratio * direction
        image = applied + ratio * image
        if step < ITERS - 2:
            rows_image = rows_applied + ratio * rows_image
            columns_image = columns_applied + ratio * columns_image
        norm_now = norm_next
    return (solution, residual)


def solution(mesh):
    placed = (
        P(("vol", "narrow"), "wide", None, None),
        P(("vol", "narrow"), "wide"),
        P(("vol", "narrow", "wide"), None),
    )
    return jax.shard_map(
        local,
        mesh=mesh,
        in_specs=placed,
        out_specs=(P(("vol", "narrow", "wide"), None), P(("vol", "narrow", "wide"), None)),
        check_vma=False,
    )
```

```python
import jax
import jax.numpy as jnp
from jax import lax
from jax.sharding import PartitionSpec as P

SEED_CLASSES = 128
ITERS = 3


SEED_WEIGHT = 2.0
PRIOR = 0.5


def sum_over(values, axes, count):
    spread = jnp.broadcast_to(values[None], (count,) + values.shape)
    return jnp.sum(lax.all_to_all(spread, axes, 0, 0, tiled=True), axis=0)


def scatter_sum(blocks, axis, count):
    if count > 4:
        return jnp.sum(lax.all_to_all(blocks, axis, 0, 0, tiled=True), axis=0)
    me = lax.axis_index(axis)
    total = lax.dynamic_index_in_dim(blocks, me, 0, keepdims=False)
    for shift in range(1, count):
        sent = lax.dynamic_index_in_dim(blocks, (me + shift) % count, 0, keepdims=False)
        pairs = [(i, (i + shift) % count) for i in range(count)]
        total = total + lax.ppermute(sent, axis, pairs)
    return total


def gather_blocks(values, axis, count):
    if count > 4:
        return lax.all_gather(values, axis, axis=0, tiled=False)
    if axis == "narrow" and count == 4:
        partner = lax.ppermute(values, axis, [(i, i ^ 1) for i in range(count)])
        both = jnp.stack([values, partner])
        return jnp.concatenate([both, lax.ppermute(both, axis, [(i, i ^ 2) for i in range(count)])])
    parts = [values]
    for shift in range(1, count):
        pairs = [(i, (i + shift) % count) for i in range(count)]
        parts.append(lax.ppermute(values, axis, pairs))
    return jnp.stack(parts)


def scatter_with(blocks, extra, axis, count):
    rows = blocks.shape[1]
    if count > 4:
        payload = jnp.concatenate(
            [blocks, jnp.broadcast_to(extra[None], (count,) + extra.shape)], axis=1
        )
        got = lax.all_to_all(payload, axis, 0, 0, tiled=True)
        return jnp.sum(got[:, :rows], axis=0), got[:, rows:]
    me = lax.axis_index(axis)
    total = lax.dynamic_index_in_dim(blocks, me, 0, keepdims=False)
    extras = [extra]
    for shift in range(1, count):
        sent = lax.dynamic_index_in_dim(blocks, (me + shift) % count, 0, keepdims=False)
        pairs = [(i, (i + shift) % count) for i in range(count)]
        got = lax.ppermute(jnp.concatenate([sent, extra], axis=0), axis, pairs)
        total = total + got[:rows]
        extras.append(got[rows:])
    return total, jnp.stack(extras)


def canonical_sum(extras, axis, count):
    if count > 4:
        return jnp.sum(extras, axis=0)
    me = lax.axis_index(axis)
    total = None
    for device in range(count):
        wanted = (me - device) % count
        term = extras[count - 1]
        for entry in range(count - 2, -1, -1):
            term = jnp.where(wanted == entry, extras[entry], term)
        total = term if total is None else total + term
    return total


def source(axis, count, entry):
    if count > 4:
        return entry
    if axis == "narrow" and count == 4:
        return lax.axis_index(axis) ^ entry
    return (lax.axis_index(axis) - entry) % count


def local(tiles, pattern, seed_label):
    groups = tiles.shape[0]
    tile = tiles.shape[2]
    own_rows = seed_label.shape[0]
    br_local = own_rows // tile
    n_wide = lax.axis_size("wide")
    n_narrow = lax.axis_size("narrow")
    n_all = n_wide * n_narrow
    width = SEED_CLASSES
    column_blocks = n_narrow * br_local
    local_column = pattern // groups * br_local + pattern % br_local
    pick = local_column[:, :, None] == jnp.arange(column_blocks, dtype=local_column.dtype)
    dense = jnp.sum(
        jnp.where(pick[:, :, None, :, None], tiles[:, :, :, None, :], 0.0), axis=1
    )
    column_sums = jnp.sum(dense, axis=(0, 1)).reshape(n_narrow, own_rows)
    order = source("wide", n_wide, jnp.arange(n_wide))
    dense = jnp.take(dense.reshape(n_wide, own_rows, column_blocks * tile), order, axis=0)
    transposed = dense.reshape(groups * tile, column_blocks * tile).T

    labels = seed_label[:, 0]
    sent_labels = labels + (column_sums[0, 0] < 0).astype(labels.dtype)
    seeded = (labels < SEED_CLASSES).astype(jnp.float32)
    fixed_column = (SEED_WEIGHT * seeded + PRIOR)[:, None]
    classes = jnp.arange(SEED_CLASSES, dtype=jnp.int32)

    def indicator(values):
        return SEED_WEIGHT * (values[..., None] == classes).astype(jnp.float32)

    def product(row_values, column_values):
        partial = jnp.dot(
            transposed, row_values.reshape(groups * tile, width), precision=lax.Precision.HIGHEST
        ).reshape(n_narrow, own_rows, width)
        quad = jnp.zeros((width,), jnp.float32)
        for entry in range(n_narrow):
            block = lax.dynamic_index_in_dim(
                partial, source("narrow", n_narrow, entry), 0, keepdims=False
            )
            quad = quad + jnp.sum(column_values[entry] * block, axis=0)
        return partial, quad

    def narrow_step(partial, partial_sums):
        weighted, extras = scatter_with(partial, partial_sums, "narrow", n_narrow)
        return weighted, canonical_sum(extras, "narrow", n_narrow)

    def wide_step(applied, narrow_sums, last):
        if last:
            sums = canonical_sum(gather_blocks(narrow_sums, "wide", n_wide), "wide", n_wide)
            return None, None, sums
        got = gather_blocks(jnp.concatenate([applied, narrow_sums], axis=0), "wide", n_wide)
        sums = canonical_sum(got[:, own_rows:], "wide", n_wide)
        return got[:, :own_rows], gather_blocks(applied, "narrow", n_narrow), sums

    rhs = indicator(labels)
    solution = jnp.zeros_like(rhs)
    residual = rhs
    direction = rhs
    rows_residual = indicator(gather_blocks(sent_labels, "wide", n_wide))
    columns_residual = indicator(gather_blocks(sent_labels, "narrow", n_narrow))
    partial, quad = product(rows_residual, columns_residual)
    degree_part = jnp.zeros((width,), jnp.float32)
    for entry in range(n_narrow):
        sums_block = lax.dynamic_index_in_dim(
            column_sums, source("narrow", n_narrow, entry), 0, keepdims=False
        )
        degree_part = degree_part + jnp.sum(
            sums_block[:, None] * columns_residual[entry] * columns_residual[entry], axis=0
        )
    partial_sums = jnp.stack(
        [
            jnp.sum(residual * residual, axis=0),
            degree_part + jnp.sum(fixed_column * direction * direction, axis=0) - quad,
        ]
    )
    carried = jnp.concatenate([partial, column_sums[:, None, :]], axis=1)
    weighted, narrow_sums = narrow_step(carried, partial_sums)
    diag_column = weighted[own_rows][:, None] + fixed_column
    image = diag_column * direction - weighted[:own_rows]
    rows_image, columns_image, first = wide_step(image, narrow_sums, ITERS == 1)
    norm_now = first[0]
    curvature = first[1]
    for step in range(ITERS):
        alpha = norm_now / curvature
        solution = solution + alpha * direction
        residual = residual - alpha * image
        if step == ITERS - 1:
            break
        rows_residual = rows_residual - alpha * rows_image
        columns_residual = columns_residual - alpha * columns_image
        partial, quad = product(rows_residual, columns_residual)
        partial_sums = jnp.stack(
            [
                jnp.sum(residual * residual, axis=0),
                jnp.sum(diag_column * residual * residual, axis=0) - quad,
                jnp.sum(residual * image, axis=0),
                jnp.sum(direction * image, axis=0),
            ]
        )
        weighted, narrow_sums = narrow_step(partial, partial_sums)
        applied = diag_column * residual - weighted
        rows_applied, columns_applied, sums = wide_step(applied, narrow_sums, step == ITERS - 2)
        norm_next = sums[0]
        ratio = norm_next / norm_now
        curvature = sums[1] + ratio * (2.0 * sums[2] + ratio * sums[3])
        direction = residual + ratio * direction
        image = applied + ratio * image
        if step < ITERS - 2:
            rows_image = rows_applied + ratio * rows_image
            columns_image = columns_applied + ratio * columns_image
        norm_now = norm_next
    return (solution, residual)


def solution(mesh):
    placed = (
        P(("vol", "narrow"), "wide", None, None),
        P(("vol", "narrow"), "wide"),
        P(("vol", "narrow", "wide"), None),
    )
    return jax.shard_map(
        local,
        mesh=mesh,
        in_specs=placed,
        out_specs=(P(("vol", "narrow", "wide"), None), P(("vol", "narrow", "wide"), None)),
        check_vma=False,
    )
```

```python
import jax
import jax.numpy as jnp
from jax import lax
from jax.sharding import PartitionSpec as P

SEED_CLASSES = 128
ITERS = 3


SEED_WEIGHT = 2.0
PRIOR = 0.5


def sum_over(values, axes, count):
    spread = jnp.broadcast_to(values[None], (count,) + values.shape)
    return jnp.sum(lax.all_to_all(spread, axes, 0, 0, tiled=True), axis=0)


def scatter_sum(blocks, axis, count):
    if count > 4:
        return jnp.sum(lax.all_to_all(blocks, axis, 0, 0, tiled=True), axis=0)
    me = lax.axis_index(axis)
    total = lax.dynamic_index_in_dim(blocks, me, 0, keepdims=False)
    for shift in range(1, count):
        sent = lax.dynamic_index_in_dim(blocks, (me + shift) % count, 0, keepdims=False)
        pairs = [(i, (i + shift) % count) for i in range(count)]
        total = total + lax.ppermute(sent, axis, pairs)
    return total


def gather_blocks(values, axis, count):
    if count > 4:
        return lax.all_gather(values, axis, axis=0, tiled=False)
    if axis == "narrow" and count == 4:
        partner = lax.ppermute(values, axis, [(i, i ^ 1) for i in range(count)])
        both = jnp.stack([values, partner])
        return jnp.concatenate([both, lax.ppermute(both, axis, [(i, i ^ 2) for i in range(count)])])
    parts = [values]
    for shift in range(1, count):
        pairs = [(i, (i + shift) % count) for i in range(count)]
        parts.append(lax.ppermute(values, axis, pairs))
    return jnp.stack(parts)


def scatter_with(blocks, extra, axis, count):
    rows = blocks.shape[1]
    if count > 4:
        payload = jnp.concatenate(
            [blocks, jnp.broadcast_to(extra[None], (count,) + extra.shape)], axis=1
        )
        got = lax.all_to_all(payload, axis, 0, 0, tiled=True)
        return jnp.sum(got[:, :rows], axis=0), got[:, rows:]
    me = lax.axis_index(axis)
    total = lax.dynamic_index_in_dim(blocks, me, 0, keepdims=False)
    extras = [extra]
    for shift in range(1, count):
        sent = lax.dynamic_index_in_dim(blocks, (me + shift) % count, 0, keepdims=False)
        pairs = [(i, (i + shift) % count) for i in range(count)]
        got = lax.ppermute(jnp.concatenate([sent, extra], axis=0), axis, pairs)
        total = total + got[:rows]
        extras.append(got[rows:])
    return total, jnp.stack(extras)


def canonical_sum(extras, axis, count):
    if count > 4:
        return jnp.sum(extras, axis=0)
    me = lax.axis_index(axis)
    total = None
    for device in range(count):
        wanted = (me - device) % count
        term = extras[count - 1]
        for entry in range(count - 2, -1, -1):
            term = jnp.where(wanted == entry, extras[entry], term)
        total = term if total is None else total + term
    return total


def source(axis, count, entry):
    if count > 4:
        return entry
    if axis == "narrow" and count == 4:
        return lax.axis_index(axis) ^ entry
    return (lax.axis_index(axis) - entry) % count


def local(tiles, pattern, seed_label):
    groups = tiles.shape[0]
    tile = tiles.shape[2]
    own_rows = seed_label.shape[0]
    br_local = own_rows // tile
    n_wide = lax.axis_size("wide")
    n_narrow = lax.axis_size("narrow")
    n_all = n_wide * n_narrow
    width = SEED_CLASSES
    column_blocks = n_narrow * br_local
    blocks_of = jnp.arange(column_blocks, dtype=pattern.dtype)
    if br_local == 1:
        low = pattern[:, :, None] >= blocks_of * groups
        pick = low & (pattern[:, :, None] < (blocks_of + 1) * groups)
    else:
        local_column = pattern // groups * br_local + pattern % br_local
        pick = local_column[:, :, None] == blocks_of
    dense = jnp.sum(
        jnp.where(pick[:, :, None, :, None], tiles[:, :, :, None, :], 0.0), axis=1
    )
    column_sums = jnp.sum(dense, axis=(0, 1)).reshape(n_narrow, own_rows)
    order = source("wide", n_wide, jnp.arange(n_wide))
    dense = jnp.take(dense.reshape(n_wide, own_rows, column_blocks * tile), order, axis=0)
    transposed = dense.reshape(groups * tile, column_blocks * tile).T

    labels = seed_label[:, 0]
    seeded = (labels < SEED_CLASSES).astype(jnp.float32)
    fixed_column = (SEED_WEIGHT * seeded + PRIOR)[:, None]
    classes = jnp.arange(SEED_CLASSES, dtype=jnp.int32)

    def indicator(values):
        return SEED_WEIGHT * (values[..., None] == classes).astype(jnp.float32)

    def product(row_values, column_values):
        partial = jnp.dot(
            transposed, row_values.reshape(groups * tile, width), precision=lax.Precision.HIGHEST
        ).reshape(n_narrow, own_rows, width)
        quad = jnp.zeros((width,), jnp.float32)
        for entry in range(n_narrow):
            block = lax.dynamic_index_in_dim(
                partial, source("narrow", n_narrow, entry), 0, keepdims=False
            )
            quad = quad + jnp.sum(column_values[entry] * block, axis=0)
        return partial, quad

    def narrow_step(partial, partial_sums):
        weighted, extras = scatter_with(partial, partial_sums, "narrow", n_narrow)
        return weighted, canonical_sum(extras, "narrow", n_narrow)

    def wide_step(applied, narrow_sums, last):
        if last:
            sums = canonical_sum(gather_blocks(narrow_sums, "wide", n_wide), "wide", n_wide)
            return None, None, sums
        got = gather_blocks(jnp.concatenate([applied, narrow_sums], axis=0), "wide", n_wide)
        sums = canonical_sum(got[:, own_rows:], "wide", n_wide)
        return got[:, :own_rows], gather_blocks(applied, "narrow", n_narrow), sums

    rhs = indicator(labels)
    solution = jnp.zeros_like(rhs)
    residual = rhs
    direction = rhs
    rows_residual = indicator(gather_blocks(labels, "wide", n_wide))
    columns_residual = indicator(gather_blocks(labels, "narrow", n_narrow))
    partial, quad = product(rows_residual, columns_residual)
    degree_part = jnp.zeros((width,), jnp.float32)
    for entry in range(n_narrow):
        sums_block = lax.dynamic_index_in_dim(
            column_sums, source("narrow", n_narrow, entry), 0, keepdims=False
        )
        degree_part = degree_part + jnp.sum(
            sums_block[:, None] * columns_residual[entry] * columns_residual[entry], axis=0
        )
    partial_sums = jnp.stack(
        [
            jnp.sum(residual * residual, axis=0),
            degree_part + jnp.sum(fixed_column * direction * direction, axis=0) - quad,
        ]
    )
    carried = jnp.concatenate([partial, column_sums[:, None, :]], axis=1)
    weighted, narrow_sums = narrow_step(carried, partial_sums)
    diag_column = weighted[own_rows][:, None] + fixed_column
    image = diag_column * direction - weighted[:own_rows]
    rows_image, columns_image, first = wide_step(image, narrow_sums, ITERS == 1)
    norm_now = first[0]
    curvature = first[1]
    for step in range(ITERS):
        alpha = norm_now / curvature
        solution = solution + alpha * direction
        residual = residual - alpha * image
        if step == ITERS - 1:
            break
        rows_residual = rows_residual - alpha * rows_image
        columns_residual = columns_residual - alpha * columns_image
        partial, quad = product(rows_residual, columns_residual)
        partial_sums = jnp.stack(
            [
                jnp.sum(residual * residual, axis=0),
                jnp.sum(diag_column * residual * residual, axis=0) - quad,
                jnp.sum(residual * image, axis=0),
                jnp.sum(direction * image, axis=0),
            ]
        )
        weighted, narrow_sums = narrow_step(partial, partial_sums)
        applied = diag_column * residual - weighted
        rows_applied, columns_applied, sums = wide_step(applied, narrow_sums, step == ITERS - 2)
        norm_next = sums[0]
        ratio = norm_next / norm_now
        curvature = sums[1] + ratio * (2.0 * sums[2] + ratio * sums[3])
        direction = residual + ratio * direction
        image = applied + ratio * image
        if step < ITERS - 2:
            rows_image = rows_applied + ratio * rows_image
            columns_image = columns_applied + ratio * columns_image
        norm_now = norm_next
    return (solution, residual)


def solution(mesh):
    placed = (
        P(("vol", "narrow"), "wide", None, None),
        P(("vol", "narrow"), "wide"),
        P(("vol", "narrow", "wide"), None),
    )
    return jax.shard_map(
        local,
        mesh=mesh,
        in_specs=placed,
        out_specs=(P(("vol", "narrow", "wide"), None), P(("vol", "narrow", "wide"), None)),
        check_vma=False,
    )
```

```python
import jax
import jax.numpy as jnp
from jax import lax
from jax.sharding import PartitionSpec as P

SEED_CLASSES = 128
ITERS = 3


SEED_WEIGHT = 2.0
PRIOR = 0.5


def sum_over(values, axes, count):
    spread = jnp.broadcast_to(values[None], (count,) + values.shape)
    return jnp.sum(lax.all_to_all(spread, axes, 0, 0, tiled=True), axis=0)


def scatter_sum(blocks, axis, count):
    if count > 4:
        return jnp.sum(lax.all_to_all(blocks, axis, 0, 0, tiled=True), axis=0)
    me = lax.axis_index(axis)
    total = lax.dynamic_index_in_dim(blocks, me, 0, keepdims=False)
    for shift in range(1, count):
        sent = lax.dynamic_index_in_dim(blocks, (me + shift) % count, 0, keepdims=False)
        pairs = [(i, (i + shift) % count) for i in range(count)]
        total = total + lax.ppermute(sent, axis, pairs)
    return total


def gather_blocks(values, axis, count):
    if count > 4:
        return lax.all_gather(values, axis, axis=0, tiled=False)
    if axis == "narrow" and count == 4:
        partner = lax.ppermute(values, axis, [(i, i ^ 1) for i in range(count)])
        both = jnp.stack([values, partner])
        return jnp.concatenate([both, lax.ppermute(both, axis, [(i, i ^ 2) for i in range(count)])])
    parts = [values]
    for shift in range(1, count):
        pairs = [(i, (i + shift) % count) for i in range(count)]
        parts.append(lax.ppermute(values, axis, pairs))
    return jnp.stack(parts)


def scatter_with(blocks, extra, axis, count):
    rows = blocks.shape[1]
    if count > 4:
        payload = jnp.concatenate(
            [blocks, jnp.broadcast_to(extra[None], (count,) + extra.shape)], axis=1
        )
        got = lax.all_to_all(payload, axis, 0, 0, tiled=True)
        return jnp.sum(got[:, :rows], axis=0), got[:, rows:]
    me = lax.axis_index(axis)
    total = lax.dynamic_index_in_dim(blocks, me, 0, keepdims=False)
    extras = [extra]
    for shift in range(1, count):
        sent = lax.dynamic_index_in_dim(blocks, (me + shift) % count, 0, keepdims=False)
        pairs = [(i, (i + shift) % count) for i in range(count)]
        got = lax.ppermute(jnp.concatenate([sent, extra], axis=0), axis, pairs)
        total = total + got[:rows]
        extras.append(got[rows:])
    return total, jnp.stack(extras)


def canonical_sum(extras, axis, count):
    if count > 4:
        return jnp.sum(extras, axis=0)
    me = lax.axis_index(axis)
    total = None
    for device in range(count):
        wanted = (me - device) % count
        term = extras[count - 1]
        for entry in range(count - 2, -1, -1):
            term = jnp.where(wanted == entry, extras[entry], term)
        total = term if total is None else total + term
    return total


def source(axis, count, entry):
    if count > 4:
        return entry
    if axis == "narrow" and count == 4:
        return lax.axis_index(axis) ^ entry
    return (lax.axis_index(axis) - entry) % count


def local(tiles, pattern, seed_label):
    groups = tiles.shape[0]
    tile = tiles.shape[2]
    own_rows = seed_label.shape[0]
    br_local = own_rows // tile
    n_wide = lax.axis_size("wide")
    n_narrow = lax.axis_size("narrow")
    n_all = n_wide * n_narrow
    width = SEED_CLASSES
    column_blocks = n_narrow * br_local
    local_column = pattern // groups * br_local + pattern % br_local
    combined = (
        jnp.zeros((groups, column_blocks, tile, tile), tiles.dtype)
        .at[jnp.arange(groups)[:, None], local_column]
        .add(tiles)
    )
    column_sums = jnp.sum(combined, axis=(0, 2)).reshape(n_narrow, own_rows)
    order = source("wide", n_wide, jnp.arange(n_wide))
    combined = jnp.take(combined.reshape(n_wide, br_local, column_blocks, tile, tile), order, axis=0)
    transposed = combined.transpose(2, 4, 0, 1, 3).reshape(column_blocks * tile, groups * tile)

    labels = seed_label[:, 0]
    seeded = (labels < SEED_CLASSES).astype(jnp.float32)
    fixed_column = (SEED_WEIGHT * seeded + PRIOR)[:, None]
    classes = jnp.arange(SEED_CLASSES, dtype=jnp.int32)

    def indicator(values):
        return SEED_WEIGHT * (values[..., None] == classes).astype(jnp.float32)

    def product(row_values, column_values):
        partial = jnp.dot(
            transposed, row_values.reshape(groups * tile, width), precision=lax.Precision.HIGHEST
        ).reshape(n_narrow, own_rows, width)
        quad = jnp.zeros((width,), jnp.float32)
        for entry in range(n_narrow):
            block = lax.dynamic_index_in_dim(
                partial, source("narrow", n_narrow, entry), 0, keepdims=False
            )
            quad = quad + jnp.sum(column_values[entry] * block, axis=0)
        return partial, quad

    def narrow_step(partial, partial_sums):
        weighted, extras = scatter_with(partial, partial_sums, "narrow", n_narrow)
        return weighted, canonical_sum(extras, "narrow", n_narrow)

    def wide_step(applied, narrow_sums, last):
        if last:
            sums = canonical_sum(gather_blocks(narrow_sums, "wide", n_wide), "wide", n_wide)
            return None, None, sums
        got = gather_blocks(jnp.concatenate([applied, narrow_sums], axis=0), "wide", n_wide)
        sums = canonical_sum(got[:, own_rows:], "wide", n_wide)
        return got[:, :own_rows], gather_blocks(applied, "narrow", n_narrow), sums

    rhs = indicator(labels)
    solution = jnp.zeros_like(rhs)
    residual = rhs
    direction = rhs
    rows_residual = indicator(gather_blocks(labels, "wide", n_wide))
    columns_residual = indicator(gather_blocks(labels, "narrow", n_narrow))
    partial, quad = product(rows_residual, columns_residual)
    degree_part = jnp.zeros((width,), jnp.float32)
    for entry in range(n_narrow):
        sums_block = lax.dynamic_index_in_dim(
            column_sums, source("narrow", n_narrow, entry), 0, keepdims=False
        )
        degree_part = degree_part + jnp.sum(
            sums_block[:, None] * columns_residual[entry] * columns_residual[entry], axis=0
        )
    partial_sums = jnp.stack(
        [
            jnp.sum(residual * residual, axis=0),
            degree_part + jnp.sum(fixed_column * direction * direction, axis=0) - quad,
        ]
    )
    carried = jnp.concatenate([partial, column_sums[:, None, :]], axis=1)
    weighted, narrow_sums = narrow_step(carried, partial_sums)
    diag_column = weighted[own_rows][:, None] + fixed_column
    image = diag_column * direction - weighted[:own_rows]
    rows_image, columns_image, first = wide_step(image, narrow_sums, ITERS == 1)
    norm_now = first[0]
    curvature = first[1]
    for step in range(ITERS):
        alpha = norm_now / curvature
        solution = solution + alpha * direction
        residual = residual - alpha * image
        if step == ITERS - 1:
            break
        rows_residual = rows_residual - alpha * rows_image
        columns_residual = columns_residual - alpha * columns_image
        partial, quad = product(rows_residual, columns_residual)
        partial_sums = jnp.stack(
            [
                jnp.sum(residual * residual, axis=0),
                jnp.sum(diag_column * residual * residual, axis=0) - quad,
                jnp.sum(residual * image, axis=0),
                jnp.sum(direction * image, axis=0),
            ]
        )
        weighted, narrow_sums = narrow_step(partial, partial_sums)
        applied = diag_column * residual - weighted
        rows_applied, columns_applied, sums = wide_step(applied, narrow_sums, step == ITERS - 2)
        norm_next = sums[0]
        ratio = norm_next / norm_now
        curvature = sums[1] + ratio * (2.0 * sums[2] + ratio * sums[3])
        direction = residual + ratio * direction
        image = applied + ratio * image
        if step < ITERS - 2:
            rows_image = rows_applied + ratio * rows_image
            columns_image = columns_applied + ratio * columns_image
        norm_now = norm_next
    return (solution, residual)


def solution(mesh):
    placed = (
        P(("vol", "narrow"), "wide", None, None),
        P(("vol", "narrow"), "wide"),
        P(("vol", "narrow", "wide"), None),
    )
    return jax.shard_map(
        local,
        mesh=mesh,
        in_specs=placed,
        out_specs=(P(("vol", "narrow", "wide"), None), P(("vol", "narrow", "wide"), None)),
        check_vma=False,
    )
```

```python
import jax
import jax.numpy as jnp
from jax import lax
from jax.sharding import PartitionSpec as P

SEED_CLASSES = 128
ITERS = 3


SEED_WEIGHT = 2.0
PRIOR = 0.5


def sum_over(values, axes, count):
    spread = jnp.broadcast_to(values[None], (count,) + values.shape)
    return jnp.sum(lax.all_to_all(spread, axes, 0, 0, tiled=True), axis=0)


def scatter_sum(blocks, axis, count):
    if count > 4:
        return jnp.sum(lax.all_to_all(blocks, axis, 0, 0, tiled=True), axis=0)
    me = lax.axis_index(axis)
    total = lax.dynamic_index_in_dim(blocks, me, 0, keepdims=False)
    for shift in range(1, count):
        sent = lax.dynamic_index_in_dim(blocks, (me + shift) % count, 0, keepdims=False)
        pairs = [(i, (i + shift) % count) for i in range(count)]
        total = total + lax.ppermute(sent, axis, pairs)
    return total


def gather_blocks(values, axis, count):
    if count > 4:
        return lax.all_gather(values, axis, axis=0, tiled=False)
    if axis == "narrow" and count == 4:
        partner = lax.ppermute(values, axis, [(i, i ^ 1) for i in range(count)])
        both = jnp.stack([values, partner])
        return jnp.concatenate([both, lax.ppermute(both, axis, [(i, i ^ 2) for i in range(count)])])
    parts = [values]
    for shift in range(1, count):
        pairs = [(i, (i + shift) % count) for i in range(count)]
        parts.append(lax.ppermute(values, axis, pairs))
    return jnp.stack(parts)


def scatter_with(blocks, extra, axis, count):
    rows = blocks.shape[1]
    if count > 4:
        payload = jnp.concatenate(
            [blocks, jnp.broadcast_to(extra[None], (count,) + extra.shape)], axis=1
        )
        got = lax.all_to_all(payload, axis, 0, 0, tiled=True)
        return jnp.sum(got[:, :rows], axis=0), got[:, rows:]
    me = lax.axis_index(axis)
    total = lax.dynamic_index_in_dim(blocks, me, 0, keepdims=False)
    extras = [extra]
    for shift in range(1, count):
        sent = lax.dynamic_index_in_dim(blocks, (me + shift) % count, 0, keepdims=False)
        pairs = [(i, (i + shift) % count) for i in range(count)]
        got = lax.ppermute(jnp.concatenate([sent, extra], axis=0), axis, pairs)
        total = total + got[:rows]
        extras.append(got[rows:])
    return total, jnp.stack(extras)


def canonical_sum(extras, axis, count):
    if count > 4:
        return jnp.sum(extras, axis=0)
    me = lax.axis_index(axis)
    total = None
    for device in range(count):
        wanted = (me - device) % count
        term = extras[count - 1]
        for entry in range(count - 2, -1, -1):
            term = jnp.where(wanted == entry, extras[entry], term)
        total = term if total is None else total + term
    return total


def source(axis, count, entry):
    if count > 4:
        return entry
    if axis == "narrow" and count == 4:
        return lax.axis_index(axis) ^ entry
    return (lax.axis_index(axis) - entry) % count


def local(tiles, pattern, seed_label):
    groups = tiles.shape[0]
    tile = tiles.shape[2]
    own_rows = seed_label.shape[0]
    br_local = own_rows // tile
    n_wide = lax.axis_size("wide")
    n_narrow = lax.axis_size("narrow")
    n_all = n_wide * n_narrow
    width = SEED_CLASSES
    column_blocks = n_narrow * br_local
    blocks_of = jnp.arange(column_blocks, dtype=pattern.dtype)
    if br_local == 1:
        low = pattern[:, :, None] >= blocks_of * groups
        pick = low & (pattern[:, :, None] < (blocks_of + 1) * groups)
    else:
        local_column = pattern // groups * br_local + pattern % br_local
        pick = local_column[:, :, None] == blocks_of
    dense = jnp.sum(
        jnp.where(pick[:, :, None, :, None], tiles[:, :, :, None, :], 0.0), axis=1
    )
    column_sums = jnp.sum(dense, axis=(0, 1)).reshape(n_narrow, own_rows)
    order = source("wide", n_wide, jnp.arange(n_wide))
    dense = jnp.take(dense.reshape(n_wide, own_rows, column_blocks * tile), order, axis=0)
    transposed = dense.reshape(groups * tile, column_blocks * tile).T

    labels = seed_label[:, 0]
    seeded = (labels < SEED_CLASSES).astype(jnp.float32)
    fixed_column = (SEED_WEIGHT * seeded + PRIOR)[:, None]
    classes = jnp.arange(SEED_CLASSES, dtype=jnp.int32)

    def indicator(values):
        return SEED_WEIGHT * (values[..., None] == classes).astype(jnp.float32)

    def product(row_values, column_values):
        partial = jnp.dot(
            transposed, row_values.reshape(groups * tile, width), precision=lax.Precision.HIGHEST
        ).reshape(n_narrow, own_rows, width)
        quad = jnp.zeros((width,), jnp.float32)
        for entry in range(n_narrow):
            block = lax.dynamic_index_in_dim(
                partial, source("narrow", n_narrow, entry), 0, keepdims=False
            )
            quad = quad + jnp.sum(column_values[entry] * block, axis=0)
        return partial, quad

    def narrow_step(partial, partial_sums):
        weighted, extras = scatter_with(partial, partial_sums, "narrow", n_narrow)
        return weighted, canonical_sum(extras, "narrow", n_narrow)

    def wide_step(applied, narrow_sums, last):
        if last:
            sums = jnp.sum(lax.all_gather(narrow_sums, "wide", axis=0, tiled=False), axis=0)
            return None, None, sums
        got = gather_blocks(jnp.concatenate([applied, narrow_sums], axis=0), "wide", n_wide)
        sums = canonical_sum(got[:, own_rows:], "wide", n_wide)
        return got[:, :own_rows], gather_blocks(applied, "narrow", n_narrow), sums

    rhs = indicator(labels)
    solution = jnp.zeros_like(rhs)
    residual = rhs
    direction = rhs
    rows_residual = indicator(gather_blocks(labels, "wide", n_wide))
    columns_residual = indicator(gather_blocks(labels, "narrow", n_narrow))
    partial, quad = product(rows_residual, columns_residual)
    degree_part = jnp.zeros((width,), jnp.float32)
    for entry in range(n_narrow):
        sums_block = lax.dynamic_index_in_dim(
            column_sums, source("narrow", n_narrow, entry), 0, keepdims=False
        )
        degree_part = degree_part + jnp.sum(
            sums_block[:, None] * columns_residual[entry] * columns_residual[entry], axis=0
        )
    partial_sums = jnp.stack(
        [
            jnp.sum(residual * residual, axis=0),
            degree_part + jnp.sum(fixed_column * direction * direction, axis=0) - quad,
        ]
    )
    carried = jnp.concatenate([partial, column_sums[:, None, :]], axis=1)
    weighted, narrow_sums = narrow_step(carried, partial_sums)
    diag_column = weighted[own_rows][:, None] + fixed_column
    image = diag_column * direction - weighted[:own_rows]
    rows_image, columns_image, first = wide_step(image, narrow_sums, ITERS == 1)
    norm_now = first[0]
    curvature = first[1]
    for step in range(ITERS):
        alpha = norm_now / curvature
        solution = solution + alpha * direction
        residual = residual - alpha * image
        if step == ITERS - 1:
            break
        rows_residual = rows_residual - alpha * rows_image
        columns_residual = columns_residual - alpha * columns_image
        partial, quad = product(rows_residual, columns_residual)
        partial_sums = jnp.stack(
            [
                jnp.sum(residual * residual, axis=0),
                jnp.sum(diag_column * residual * residual, axis=0) - quad,
                jnp.sum(residual * image, axis=0),
                jnp.sum(direction * image, axis=0),
            ]
        )
        weighted, narrow_sums = narrow_step(partial, partial_sums)
        applied = diag_column * residual - weighted
        rows_applied, columns_applied, sums = wide_step(applied, narrow_sums, step == ITERS - 2)
        norm_next = sums[0]
        ratio = norm_next / norm_now
        curvature = sums[1] + ratio * (2.0 * sums[2] + ratio * sums[3])
        direction = residual + ratio * direction
        image = applied + ratio * image
        if step < ITERS - 2:
            rows_image = rows_applied + ratio * rows_image
            columns_image = columns_applied + ratio * columns_image
        norm_now = norm_next
    return (solution, residual)


def solution(mesh):
    placed = (
        P(("vol", "narrow"), "wide", None, None),
        P(("vol", "narrow"), "wide"),
        P(("vol", "narrow", "wide"), None),
    )
    return jax.shard_map(
        local,
        mesh=mesh,
        in_specs=placed,
        out_specs=(P(("vol", "narrow", "wide"), None), P(("vol", "narrow", "wide"), None)),
        check_vma=False,
    )
```

```python
import jax
import jax.numpy as jnp
from jax import lax
from jax.sharding import PartitionSpec as P

SEED_CLASSES = 128
ITERS = 3


SEED_WEIGHT = 2.0
PRIOR = 0.5


def sum_over(values, axes, count):
    spread = jnp.broadcast_to(values[None], (count,) + values.shape)
    return jnp.sum(lax.all_to_all(spread, axes, 0, 0, tiled=True), axis=0)


def scatter_sum(blocks, axis, count):
    if count > 4:
        return jnp.sum(lax.all_to_all(blocks, axis, 0, 0, tiled=True), axis=0)
    me = lax.axis_index(axis)
    total = lax.dynamic_index_in_dim(blocks, me, 0, keepdims=False)
    for shift in range(1, count):
        sent = lax.dynamic_index_in_dim(blocks, (me + shift) % count, 0, keepdims=False)
        pairs = [(i, (i + shift) % count) for i in range(count)]
        total = total + lax.ppermute(sent, axis, pairs)
    return total


def gather_blocks(values, axis, count):
    if count > 4:
        return lax.all_gather(values, axis, axis=0, tiled=False)
    if axis == "narrow" and count == 4:
        partner = lax.ppermute(values, axis, [(i, i ^ 1) for i in range(count)])
        both = jnp.stack([values, partner])
        return jnp.concatenate([both, lax.ppermute(both, axis, [(i, i ^ 2) for i in range(count)])])
    if axis == "wide" and count == 4:
        parts = [values]
        for mask in range(1, count):
            parts.append(lax.ppermute(values, axis, [(i, i ^ mask) for i in range(count)]))
        return jnp.stack(parts)
    parts = [values]
    for shift in range(1, count):
        pairs = [(i, (i + shift) % count) for i in range(count)]
        parts.append(lax.ppermute(values, axis, pairs))
    return jnp.stack(parts)


def scatter_with(blocks, extra, axis, count):
    rows = blocks.shape[1]
    if count > 4:
        payload = jnp.concatenate(
            [blocks, jnp.broadcast_to(extra[None], (count,) + extra.shape)], axis=1
        )
        got = lax.all_to_all(payload, axis, 0, 0, tiled=True)
        return jnp.sum(got[:, :rows], axis=0), got[:, rows:]
    me = lax.axis_index(axis)
    total = lax.dynamic_index_in_dim(blocks, me, 0, keepdims=False)
    extras = [extra]
    for shift in range(1, count):
        sent = lax.dynamic_index_in_dim(blocks, (me + shift) % count, 0, keepdims=False)
        pairs = [(i, (i + shift) % count) for i in range(count)]
        got = lax.ppermute(jnp.concatenate([sent, extra], axis=0), axis, pairs)
        total = total + got[:rows]
        extras.append(got[rows:])
    return total, jnp.stack(extras)


def canonical_sum(extras, axis, count, shifted):
    if count > 4:
        return jnp.sum(extras, axis=0)
    me = lax.axis_index(axis)
    total = None
    for device in range(count):
        wanted = (me - device) % count if shifted else source(axis, count, device)
        term = extras[count - 1]
        for entry in range(count - 2, -1, -1):
            term = jnp.where(wanted == entry, extras[entry], term)
        total = term if total is None else total + term
    return total


def source(axis, count, entry):
    if count > 4:
        return entry
    if count == 4:
        return lax.axis_index(axis) ^ entry
    return (lax.axis_index(axis) - entry) % count


def local(tiles, pattern, seed_label):
    groups = tiles.shape[0]
    tile = tiles.shape[2]
    own_rows = seed_label.shape[0]
    br_local = own_rows // tile
    n_wide = lax.axis_size("wide")
    n_narrow = lax.axis_size("narrow")
    n_all = n_wide * n_narrow
    width = SEED_CLASSES
    column_blocks = n_narrow * br_local
    blocks_of = jnp.arange(column_blocks, dtype=pattern.dtype)
    if br_local == 1:
        low = pattern[:, :, None] >= blocks_of * groups
        pick = low & (pattern[:, :, None] < (blocks_of + 1) * groups)
    else:
        local_column = pattern // groups * br_local + pattern % br_local
        pick = local_column[:, :, None] == blocks_of
    dense = jnp.sum(
        jnp.where(pick[:, :, None, :, None], tiles[:, :, :, None, :], 0.0), axis=1
    )
    column_sums = jnp.sum(dense, axis=(0, 1)).reshape(n_narrow, own_rows)
    order = source("wide", n_wide, jnp.arange(n_wide))
    dense = jnp.take(dense.reshape(n_wide, own_rows, column_blocks * tile), order, axis=0)
    transposed = dense.reshape(groups * tile, column_blocks * tile).T

    labels = seed_label[:, 0]
    seeded = (labels < SEED_CLASSES).astype(jnp.float32)
    fixed_column = (SEED_WEIGHT * seeded + PRIOR)[:, None]
    classes = jnp.arange(SEED_CLASSES, dtype=jnp.int32)

    def indicator(values):
        return SEED_WEIGHT * (values[..., None] == classes).astype(jnp.float32)

    def product(row_values, column_values):
        partial = jnp.dot(
            transposed, row_values.reshape(groups * tile, width), precision=lax.Precision.HIGHEST
        ).reshape(n_narrow, own_rows, width)
        quad = jnp.zeros((width,), jnp.float32)
        for entry in range(n_narrow):
            block = lax.dynamic_index_in_dim(
                partial, source("narrow", n_narrow, entry), 0, keepdims=False
            )
            quad = quad + jnp.sum(column_values[entry] * block, axis=0)
        return partial, quad

    def narrow_step(partial, partial_sums):
        weighted, extras = scatter_with(partial, partial_sums, "narrow", n_narrow)
        return weighted, canonical_sum(extras, "narrow", n_narrow, True)

    def wide_step(applied, narrow_sums, last):
        if last:
            sums = canonical_sum(gather_blocks(narrow_sums, "wide", n_wide), "wide", n_wide, False)
            return None, None, sums
        got = gather_blocks(jnp.concatenate([applied, narrow_sums], axis=0), "wide", n_wide)
        sums = canonical_sum(got[:, own_rows:], "wide", n_wide, False)
        return got[:, :own_rows], gather_blocks(applied, "narrow", n_narrow), sums

    rhs = indicator(labels)
    solution = jnp.zeros_like(rhs)
    residual = rhs
    direction = rhs
    rows_residual = indicator(gather_blocks(labels, "wide", n_wide))
    columns_residual = indicator(gather_blocks(labels, "narrow", n_narrow))
    partial, quad = product(rows_residual, columns_residual)
    degree_part = jnp.zeros((width,), jnp.float32)
    for entry in range(n_narrow):
        sums_block = lax.dynamic_index_in_dim(
            column_sums, source("narrow", n_narrow, entry), 0, keepdims=False
        )
        degree_part = degree_part + jnp.sum(
            sums_block[:, None] * columns_residual[entry] * columns_residual[entry], axis=0
        )
    partial_sums = jnp.stack(
        [
            jnp.sum(residual * residual, axis=0),
            degree_part + jnp.sum(fixed_column * direction * direction, axis=0) - quad,
        ]
    )
    carried = jnp.concatenate([partial, column_sums[:, None, :]], axis=1)
    weighted, narrow_sums = narrow_step(carried, partial_sums)
    diag_column = weighted[own_rows][:, None] + fixed_column
    image = diag_column * direction - weighted[:own_rows]
    rows_image, columns_image, first = wide_step(image, narrow_sums, ITERS == 1)
    norm_now = first[0]
    curvature = first[1]
    for step in range(ITERS):
        alpha = norm_now / curvature
        solution = solution + alpha * direction
        residual = residual - alpha * image
        if step == ITERS - 1:
            break
        rows_residual = rows_residual - alpha * rows_image
        columns_residual = columns_residual - alpha * columns_image
        partial, quad = product(rows_residual, columns_residual)
        partial_sums = jnp.stack(
            [
                jnp.sum(residual * residual, axis=0),
                jnp.sum(diag_column * residual * residual, axis=0) - quad,
                jnp.sum(residual * image, axis=0),
                jnp.sum(direction * image, axis=0),
            ]
        )
        weighted, narrow_sums = narrow_step(partial, partial_sums)
        applied = diag_column * residual - weighted
        rows_applied, columns_applied, sums = wide_step(applied, narrow_sums, step == ITERS - 2)
        norm_next = sums[0]
        ratio = norm_next / norm_now
        curvature = sums[1] + ratio * (2.0 * sums[2] + ratio * sums[3])
        direction = residual + ratio * direction
        image = applied + ratio * image
        if step < ITERS - 2:
            rows_image = rows_applied + ratio * rows_image
            columns_image = columns_applied + ratio * columns_image
        norm_now = norm_next
    return (solution, residual)


def solution(mesh):
    placed = (
        P(("vol", "narrow"), "wide", None, None),
        P(("vol", "narrow"), "wide"),
        P(("vol", "narrow", "wide"), None),
    )
    return jax.shard_map(
        local,
        mesh=mesh,
        in_specs=placed,
        out_specs=(P(("vol", "narrow", "wide"), None), P(("vol", "narrow", "wide"), None)),
        check_vma=False,
    )
```

```python
import jax
import jax.numpy as jnp
from jax import lax
from jax.sharding import PartitionSpec as P

SEED_CLASSES = 128
ITERS = 3


SEED_WEIGHT = 2.0
PRIOR = 0.5


def sum_over(values, axes, count):
    spread = jnp.broadcast_to(values[None], (count,) + values.shape)
    return jnp.sum(lax.all_to_all(spread, axes, 0, 0, tiled=True), axis=0)


def scatter_sum(blocks, axis, count):
    if count > 4:
        return jnp.sum(lax.all_to_all(blocks, axis, 0, 0, tiled=True), axis=0)
    me = lax.axis_index(axis)
    total = lax.dynamic_index_in_dim(blocks, me, 0, keepdims=False)
    for shift in range(1, count):
        sent = lax.dynamic_index_in_dim(blocks, (me + shift) % count, 0, keepdims=False)
        pairs = [(i, (i + shift) % count) for i in range(count)]
        total = total + lax.ppermute(sent, axis, pairs)
    return total


def gather_blocks(values, axis, count):
    if count > 4:
        return lax.all_gather(values, axis, axis=0, tiled=False)
    if axis == "narrow" and count == 4:
        partner = lax.ppermute(values, axis, [(i, i ^ 2) for i in range(count)])
        both = jnp.stack([values, partner])
        return jnp.concatenate([both, lax.ppermute(both, axis, [(i, i ^ 1) for i in range(count)])])
    parts = [values]
    for shift in range(1, count):
        pairs = [(i, (i + shift) % count) for i in range(count)]
        parts.append(lax.ppermute(values, axis, pairs))
    return jnp.stack(parts)


def scatter_with(blocks, extra, axis, count):
    rows = blocks.shape[1]
    if count > 4:
        payload = jnp.concatenate(
            [blocks, jnp.broadcast_to(extra[None], (count,) + extra.shape)], axis=1
        )
        got = lax.all_to_all(payload, axis, 0, 0, tiled=True)
        return jnp.sum(got[:, :rows], axis=0), got[:, rows:]
    me = lax.axis_index(axis)
    total = lax.dynamic_index_in_dim(blocks, me, 0, keepdims=False)
    extras = [extra]
    for shift in range(1, count):
        sent = lax.dynamic_index_in_dim(blocks, (me + shift) % count, 0, keepdims=False)
        pairs = [(i, (i + shift) % count) for i in range(count)]
        got = lax.ppermute(jnp.concatenate([sent, extra], axis=0), axis, pairs)
        total = total + got[:rows]
        extras.append(got[rows:])
    return total, jnp.stack(extras)


def canonical_sum(extras, axis, count):
    if count > 4:
        return jnp.sum(extras, axis=0)
    me = lax.axis_index(axis)
    total = None
    for device in range(count):
        wanted = (me - device) % count
        term = extras[count - 1]
        for entry in range(count - 2, -1, -1):
            term = jnp.where(wanted == entry, extras[entry], term)
        total = term if total is None else total + term
    return total


def source(axis, count, entry):
    if count > 4:
        return entry
    if axis == "narrow" and count == 4:
        return lax.axis_index(axis) ^ (entry % 2 * 2 + entry // 2)
    return (lax.axis_index(axis) - entry) % count


def local(tiles, pattern, seed_label):
    groups = tiles.shape[0]
    tile = tiles.shape[2]
    own_rows = seed_label.shape[0]
    br_local = own_rows // tile
    n_wide = lax.axis_size("wide")
    n_narrow = lax.axis_size("narrow")
    n_all = n_wide * n_narrow
    width = SEED_CLASSES
    column_blocks = n_narrow * br_local
    blocks_of = jnp.arange(column_blocks, dtype=pattern.dtype)
    if br_local == 1:
        low = pattern[:, :, None] >= blocks_of * groups
        pick = low & (pattern[:, :, None] < (blocks_of + 1) * groups)
    else:
        local_column = pattern // groups * br_local + pattern % br_local
        pick = local_column[:, :, None] == blocks_of
    dense = jnp.sum(
        jnp.where(pick[:, :, None, :, None], tiles[:, :, :, None, :], 0.0), axis=1
    )
    column_sums = jnp.sum(dense, axis=(0, 1)).reshape(n_narrow, own_rows)
    order = source("wide", n_wide, jnp.arange(n_wide))
    dense = jnp.take(dense.reshape(n_wide, own_rows, column_blocks * tile), order, axis=0)
    transposed = dense.reshape(groups * tile, column_blocks * tile).T

    labels = seed_label[:, 0]
    seeded = (labels < SEED_CLASSES).astype(jnp.float32)
    fixed_column = (SEED_WEIGHT * seeded + PRIOR)[:, None]
    classes = jnp.arange(SEED_CLASSES, dtype=jnp.int32)

    def indicator(values):
        return SEED_WEIGHT * (values[..., None] == classes).astype(jnp.float32)

    def product(row_values, column_values):
        partial = jnp.dot(
            transposed, row_values.reshape(groups * tile, width), precision=lax.Precision.HIGHEST
        ).reshape(n_narrow, own_rows, width)
        quad = jnp.zeros((width,), jnp.float32)
        for entry in range(n_narrow):
            block = lax.dynamic_index_in_dim(
                partial, source("narrow", n_narrow, entry), 0, keepdims=False
            )
            quad = quad + jnp.sum(column_values[entry] * block, axis=0)
        return partial, quad

    def narrow_step(partial, partial_sums):
        weighted, extras = scatter_with(partial, partial_sums, "narrow", n_narrow)
        return weighted, canonical_sum(extras, "narrow", n_narrow)

    def wide_step(applied, narrow_sums, last):
        if last:
            sums = canonical_sum(gather_blocks(narrow_sums, "wide", n_wide), "wide", n_wide)
            return None, None, sums
        got = gather_blocks(jnp.concatenate([applied, narrow_sums], axis=0), "wide", n_wide)
        sums = canonical_sum(got[:, own_rows:], "wide", n_wide)
        return got[:, :own_rows], gather_blocks(applied, "narrow", n_narrow), sums

    rhs = indicator(labels)
    solution = jnp.zeros_like(rhs)
    residual = rhs
    direction = rhs
    rows_residual = indicator(gather_blocks(labels, "wide", n_wide))
    columns_residual = indicator(gather_blocks(labels, "narrow", n_narrow))
    partial, quad = product(rows_residual, columns_residual)
    degree_part = jnp.zeros((width,), jnp.float32)
    for entry in range(n_narrow):
        sums_block = lax.dynamic_index_in_dim(
            column_sums, source("narrow", n_narrow, entry), 0, keepdims=False
        )
        degree_part = degree_part + jnp.sum(
            sums_block[:, None] * columns_residual[entry] * columns_residual[entry], axis=0
        )
    partial_sums = jnp.stack(
        [
            jnp.sum(residual * residual, axis=0),
            degree_part + jnp.sum(fixed_column * direction * direction, axis=0) - quad,
        ]
    )
    carried = jnp.concatenate([partial, column_sums[:, None, :]], axis=1)
    weighted, narrow_sums = narrow_step(carried, partial_sums)
    diag_column = weighted[own_rows][:, None] + fixed_column
    image = diag_column * direction - weighted[:own_rows]
    rows_image, columns_image, first = wide_step(image, narrow_sums, ITERS == 1)
    norm_now = first[0]
    curvature = first[1]
    for step in range(ITERS):
        alpha = norm_now / curvature
        solution = solution + alpha * direction
        residual = residual - alpha * image
        if step == ITERS - 1:
            break
        rows_residual = rows_residual - alpha * rows_image
        columns_residual = columns_residual - alpha * columns_image
        partial, quad = product(rows_residual, columns_residual)
        partial_sums = jnp.stack(
            [
                jnp.sum(residual * residual, axis=0),
                jnp.sum(diag_column * residual * residual, axis=0) - quad,
                jnp.sum(residual * image, axis=0),
                jnp.sum(direction * image, axis=0),
            ]
        )
        weighted, narrow_sums = narrow_step(partial, partial_sums)
        applied = diag_column * residual - weighted
        rows_applied, columns_applied, sums = wide_step(applied, narrow_sums, step == ITERS - 2)
        norm_next = sums[0]
        ratio = norm_next / norm_now
        curvature = sums[1] + ratio * (2.0 * sums[2] + ratio * sums[3])
        direction = residual + ratio * direction
        image = applied + ratio * image
        if step < ITERS - 2:
            rows_image = rows_applied + ratio * rows_image
            columns_image = columns_applied + ratio * columns_image
        norm_now = norm_next
    return (solution, residual)


def solution(mesh):
    placed = (
        P(("vol", "narrow"), "wide", None, None),
        P(("vol", "narrow"), "wide"),
        P(("vol", "narrow", "wide"), None),
    )
    return jax.shard_map(
        local,
        mesh=mesh,
        in_specs=placed,
        out_specs=(P(("vol", "narrow", "wide"), None), P(("vol", "narrow", "wide"), None)),
        check_vma=False,
    )
```

```python
import jax
import jax.numpy as jnp
from jax import lax
from jax.sharding import PartitionSpec as P

SEED_CLASSES = 128
ITERS = 3


SEED_WEIGHT = 2.0
PRIOR = 0.5


def sum_over(values, axes, count):
    spread = jnp.broadcast_to(values[None], (count,) + values.shape)
    return jnp.sum(lax.all_to_all(spread, axes, 0, 0, tiled=True), axis=0)


def scatter_sum(blocks, axis, count):
    if count > 4:
        return jnp.sum(lax.all_to_all(blocks, axis, 0, 0, tiled=True), axis=0)
    me = lax.axis_index(axis)
    total = lax.dynamic_index_in_dim(blocks, me, 0, keepdims=False)
    for shift in range(1, count):
        sent = lax.dynamic_index_in_dim(blocks, (me + shift) % count, 0, keepdims=False)
        pairs = [(i, (i + shift) % count) for i in range(count)]
        total = total + lax.ppermute(sent, axis, pairs)
    return total


def gather_blocks(values, axis, count):
    if count > 4:
        return lax.all_gather(values, axis, axis=0, tiled=False)
    if axis == "narrow" and count == 4:
        partner = lax.ppermute(values, axis, [(i, i ^ 1) for i in range(count)])
        both = jnp.stack([values, partner])
        return jnp.concatenate([both, lax.ppermute(both, axis, [(i, i ^ 2) for i in range(count)])])
    parts = [values]
    for shift in range(1, count):
        pairs = [(i, (i + shift) % count) for i in range(count)]
        parts.append(lax.ppermute(values, axis, pairs))
    return jnp.stack(parts)


def scatter_with(blocks, extra, axis, count):
    rows = blocks.shape[1]
    if count > 4:
        payload = jnp.concatenate(
            [blocks, jnp.broadcast_to(extra[None], (count,) + extra.shape)], axis=1
        )
        got = lax.all_to_all(payload, axis, 0, 0, tiled=True)
        return jnp.sum(got[:, :rows], axis=0), got[:, rows:]
    me = lax.axis_index(axis)
    total = lax.dynamic_index_in_dim(blocks, me, 0, keepdims=False)
    extras = [extra]
    for shift in range(1, count):
        target = me ^ shift if count == 4 else (me + shift) % count
        sent = lax.dynamic_index_in_dim(blocks, target, 0, keepdims=False)
        if count == 4:
            pairs = [(i, i ^ shift) for i in range(count)]
        else:
            pairs = [(i, (i + shift) % count) for i in range(count)]
        got = lax.ppermute(jnp.concatenate([sent, extra], axis=0), axis, pairs)
        total = total + got[:rows]
        extras.append(got[rows:])
    return total, jnp.stack(extras)


def canonical_sum(extras, axis, count, paired=False):
    if count > 4:
        return jnp.sum(extras, axis=0)
    me = lax.axis_index(axis)
    total = None
    for device in range(count):
        wanted = me ^ device if paired and count == 4 else (me - device) % count
        term = extras[count - 1]
        for entry in range(count - 2, -1, -1):
            term = jnp.where(wanted == entry, extras[entry], term)
        total = term if total is None else total + term
    return total


def source(axis, count, entry):
    if count > 4:
        return entry
    if axis == "narrow" and count == 4:
        return lax.axis_index(axis) ^ entry
    return (lax.axis_index(axis) - entry) % count


def local(tiles, pattern, seed_label):
    groups = tiles.shape[0]
    tile = tiles.shape[2]
    own_rows = seed_label.shape[0]
    br_local = own_rows // tile
    n_wide = lax.axis_size("wide")
    n_narrow = lax.axis_size("narrow")
    n_all = n_wide * n_narrow
    width = SEED_CLASSES
    column_blocks = n_narrow * br_local
    blocks_of = jnp.arange(column_blocks, dtype=pattern.dtype)
    if br_local == 1:
        low = pattern[:, :, None] >= blocks_of * groups
        pick = low & (pattern[:, :, None] < (blocks_of + 1) * groups)
    else:
        local_column = pattern // groups * br_local + pattern % br_local
        pick = local_column[:, :, None] == blocks_of
    dense = jnp.sum(
        jnp.where(pick[:, :, None, :, None], tiles[:, :, :, None, :], 0.0), axis=1
    )
    column_sums = jnp.sum(dense, axis=(0, 1)).reshape(n_narrow, own_rows)
    order = source("wide", n_wide, jnp.arange(n_wide))
    dense = jnp.take(dense.reshape(n_wide, own_rows, column_blocks * tile), order, axis=0)
    transposed = dense.reshape(groups * tile, column_blocks * tile).T

    labels = seed_label[:, 0]
    seeded = (labels < SEED_CLASSES).astype(jnp.float32)
    fixed_column = (SEED_WEIGHT * seeded + PRIOR)[:, None]
    classes = jnp.arange(SEED_CLASSES, dtype=jnp.int32)

    def indicator(values):
        return SEED_WEIGHT * (values[..., None] == classes).astype(jnp.float32)

    def product(row_values, column_values):
        partial = jnp.dot(
            transposed, row_values.reshape(groups * tile, width), precision=lax.Precision.HIGHEST
        ).reshape(n_narrow, own_rows, width)
        quad = jnp.zeros((width,), jnp.float32)
        for entry in range(n_narrow):
            block = lax.dynamic_index_in_dim(
                partial, source("narrow", n_narrow, entry), 0, keepdims=False
            )
            quad = quad + jnp.sum(column_values[entry] * block, axis=0)
        return partial, quad

    def narrow_step(partial, partial_sums):
        weighted, extras = scatter_with(partial, partial_sums, "narrow", n_narrow)
        return weighted, canonical_sum(extras, "narrow", n_narrow, paired=True)

    def wide_step(applied, narrow_sums, last):
        if last:
            sums = canonical_sum(gather_blocks(narrow_sums, "wide", n_wide), "wide", n_wide)
            return None, None, sums
        got = gather_blocks(jnp.concatenate([applied, narrow_sums], axis=0), "wide", n_wide)
        sums = canonical_sum(got[:, own_rows:], "wide", n_wide)
        return got[:, :own_rows], gather_blocks(applied, "narrow", n_narrow), sums

    rhs = indicator(labels)
    solution = jnp.zeros_like(rhs)
    residual = rhs
    direction = rhs
    rows_residual = indicator(gather_blocks(labels, "wide", n_wide))
    columns_residual = indicator(gather_blocks(labels, "narrow", n_narrow))
    partial, quad = product(rows_residual, columns_residual)
    degree_part = jnp.zeros((width,), jnp.float32)
    for entry in range(n_narrow):
        sums_block = lax.dynamic_index_in_dim(
            column_sums, source("narrow", n_narrow, entry), 0, keepdims=False
        )
        degree_part = degree_part + jnp.sum(
            sums_block[:, None] * columns_residual[entry] * columns_residual[entry], axis=0
        )
    partial_sums = jnp.stack(
        [
            jnp.sum(residual * residual, axis=0),
            degree_part + jnp.sum(fixed_column * direction * direction, axis=0) - quad,
        ]
    )
    carried = jnp.concatenate([partial, column_sums[:, None, :]], axis=1)
    weighted, narrow_sums = narrow_step(carried, partial_sums)
    diag_column = weighted[own_rows][:, None] + fixed_column
    image = diag_column * direction - weighted[:own_rows]
    rows_image, columns_image, first = wide_step(image, narrow_sums, ITERS == 1)
    norm_now = first[0]
    curvature = first[1]
    for step in range(ITERS):
        alpha = norm_now / curvature
        solution = solution + alpha * direction
        residual = residual - alpha * image
        if step == ITERS - 1:
            break
        rows_residual = rows_residual - alpha * rows_image
        columns_residual = columns_residual - alpha * columns_image
        partial, quad = product(rows_residual, columns_residual)
        partial_sums = jnp.stack(
            [
                jnp.sum(residual * residual, axis=0),
                jnp.sum(diag_column * residual * residual, axis=0) - quad,
                jnp.sum(residual * image, axis=0),
                jnp.sum(direction * image, axis=0),
            ]
        )
        weighted, narrow_sums = narrow_step(partial, partial_sums)
        applied = diag_column * residual - weighted
        rows_applied, columns_applied, sums = wide_step(applied, narrow_sums, step == ITERS - 2)
        norm_next = sums[0]
        ratio = norm_next / norm_now
        curvature = sums[1] + ratio * (2.0 * sums[2] + ratio * sums[3])
        direction = residual + ratio * direction
        image = applied + ratio * image
        if step < ITERS - 2:
            rows_image = rows_applied + ratio * rows_image
            columns_image = columns_applied + ratio * columns_image
        norm_now = norm_next
    return (solution, residual)


def solution(mesh):
    placed = (
        P(("vol", "narrow"), "wide", None, None),
        P(("vol", "narrow"), "wide"),
        P(("vol", "narrow", "wide"), None),
    )
    return jax.shard_map(
        local,
        mesh=mesh,
        in_specs=placed,
        out_specs=(P(("vol", "narrow", "wide"), None), P(("vol", "narrow", "wide"), None)),
        check_vma=False,
    )
```
